128 devices in a mesh: seq: 16 (over y, x), grp: 8 (over z, core).
Axes of the slice: x: 4, y: 4, z: 4, core: 2. Of those that a mesh axis runs over, the one named last changes fastest.
Arguments:
- patches: bfloat16 [16384, 1664], P(('grp', 'seq')), may hold values from -6 to 6
- vis_gain: float32 [1664], replicated, may hold values from 0.25 to 1.75
- vis_qkv: bfloat16 [3, 1664, 1664], P(None, None, 'seq')
- vis_out: bfloat16 [1664, 1664], P('seq'), may hold values from -0.15625 to 0.15625
- merge_gain: float32 [1664], replicated, may hold values from 0.25 to 1.75
- merge_w: bfloat16 [6656, 1664], P('seq'), may hold values from -0.078125 to 0.078125
- image_blocks: int32 [8, 4], P('grp'), may hold values from 1 to 256, 512 in all within a row
- dest_group: int32 [4096, 1], P(('grp', 'seq')), may hold values from 0 to 7; in each aligned block of 32 rows (0 to 31, 32 to 63, ...) at most 8 rows name the same one
- slot_rows: int32 [8, 16, 128], P('grp', 'seq'), may hold values from 0 to 127, each once within a row
- prompt_len: int32 [8], P('grp'), may hold values from 512 to 2048
- text_emb: bfloat16 [16384, 1664], P(('grp', 'seq')), may hold values from -6 to 6
- txt_gain: float32 [1664], replicated, may hold values from 0.25 to 1.75
- txt_qkv: bfloat16 [3, 1664, 1664], P(None, None, 'seq')
- txt_out: bfloat16 [1664, 1664], P('seq'), may hold values from -0.15625 to 0.15625
Outputs:
- text_out: float32 [16384, 1664], P(('grp', 'seq'))
The draws below stay inside these ranges and needn't reach their ends.
Inputs may be any that keep to these rules, and one draw needn't show every extreme that they name: image_blocks[g] sum to 512; one image of every group has the most. `dest_group`: of the 32 merged tokens of one device (aligned blocks of rows), at most 8 name one group. slot_rows[q, s] is a permutation of 0 to 127.
All inputs are finite; a program needn't handle non-finite values.
Results may differ from the reference program's by a relative error of at most 0.012.
Values may be sent and summed in bfloat16 or wider, within the bound.
No kernel may reach another device: no remote copies, remote signals or barrier semaphores. Data moves between devices by JAX's collectives and lax.ppermute only.
A program may use at most 64 MiB of HBM per device.

```python
import math
import jax
import jax.numpy as jnp
import numpy as np
from jax import lax

D = 1664
HEADS = 16
HEAD_DIM = 104
TXT_DEV = 128
IMGS = 4
MRG = 6656
VT = 2048
PT = 2048
MT = 32
MTOT = 4096
CAP = 8
VIS_ALL = 16384
TXT_ALL = 16384
N_SEQ = 16
N_GRP = 8


def qkv_draw(key, salt):
    folded = jax.random.fold_in(key, salt)
    stacked = jax.random.normal(folded, (3, D, D), jnp.float32) * D ** (-0.5)
    return stacked.astype(jnp.bfloat16)


def draw_vis_qkv(key, part):
    return qkv_draw(key, 11)


def draw_txt_qkv(key, part):
    return qkv_draw(key, 12)


def touch_ends(drawn, own_key, least, top_value):
    longest = drawn.shape.index(max(drawn.shape))
    spots = []
    for shift in (0, 1):
        where = [jax.random.randint(jax.random.fold_in(own_key, axis), (), 0, length) for axis, length in enumerate(drawn.shape)]
        where[longest] = (where[longest] + shift) % drawn.shape[longest]
        spots.append(tuple(where))
    return drawn.at[spots[0]].set(least).at[spots[1]].set(top_value)


def levels(key, extent, cuts, least, high):
    loudness = 1.0
    for position, blocks in cuts:
        draws = jax.random.uniform(jax.random.fold_in(jax.random.fold_in(key, 6), position), (blocks,), jnp.float32, least / len(cuts), high / len(cuts))
        loudness = loudness * jnp.repeat(jnp.exp(draws), extent[position] // blocks).reshape((-1,) + (1,) * (len(extent) - 1 - position))
    return loudness


def length_profile(amount, total, most, lean):
    loads = [(1 << 20) // math.isqrt(rank ** lean) + 1 for rank in range(2, amount + 1)]
    rest, counts = total - most - (amount - 1), [1] * (amount - 1)
    while rest > 0:
        free = [i for i in range(amount - 1) if counts[i] < most]
        mass, left = sum([loads[i] for i in free]), rest
        for i in free:
            addition = min(most - counts[i], max(1, left * loads[i] // mass), rest)
            counts[i] = counts[i] + addition
            rest = rest - addition
    return np.array([most] + counts)


def ragged(key, amount, total, most, lean):
    if amount == 2:
        one = jax.random.randint(key, (), max(1, total - most), min(most, total - 1) + 1)
        return jnp.stack([one, total - one])
    sizes = jnp.asarray(length_profile(amount, total, most, lean), jnp.int32)
    twos = (amount - 1) // 2
    donor, receiver = sizes[1:1 + 2 * twos:2], sizes[2:2 + 2 * twos:2]
    slack = jnp.minimum(donor - 1, most - receiver)
    shifted = jax.random.randint(jax.random.fold_in(key, 1), (twos,), 0, 1 << 20) % (slack + 1)
    sizes = sizes.at[1:1 + 2 * twos:2].set(donor - shifted).at[2:2 + 2 * twos:2].set(receiver + shifted)
    return sizes[jax.random.permutation(jax.random.fold_in(key, 2), amount)]


def routed_block(key, own, number, rows, number_of, top, bound, slope):
    sequence = jax.random.permutation(key, number_of)
    packed, usual = portions_of(number_of, rows * top, bound, slope, True), portions_of(number_of, rows * top, bound, slope, False)
    places = jnp.arange(number_of)

    def named(lengths, turn):
        used = int((lengths > 0).sum())
        fixed = max(1, used // 4)
        moved = fixed + (places - fixed + turn * (used - fixed)) % max(1, number_of - fixed)
        return jnp.zeros((number_of,), jnp.int32).at[sequence[jnp.where(places < fixed, places, moved)]].set(jnp.asarray(lengths, jnp.int32))

    lengths = jnp.where(number % 4 == 0, named(packed, number // 4), named(usual, number - number // 4 - 1))
    mixed = jax.random.permutation(jax.random.fold_in(own, 3), number_of)
    source_of, receiver = mixed[0:number_of // 2 * 2:2], mixed[1:number_of // 2 * 2:2]
    room = jnp.minimum(lengths[source_of] - 1, bound - lengths[receiver]) // 2
    room = jnp.where((source_of == sequence[0]) | (receiver == sequence[0]) | (lengths[receiver] == 0), 0, jnp.maximum(room, 0))
    moved = jax.random.randint(jax.random.fold_in(own, 4), (number_of // 2,), 0, 1 << 20) % (room + 1)
    lengths = lengths.at[source_of].add(-moved).at[receiver].add(moved)
    items = jnp.searchsorted(jnp.cumsum(lengths), jnp.arange(rows * top), side="right").astype(jnp.int32)
    table = items.reshape(top, rows).T
    table = table[jax.random.permutation(jax.random.fold_in(own, 1), rows)]
    turn = jax.random.randint(jax.random.fold_in(own, 2), (rows, 1), 0, top)
    return jnp.take_along_axis(table, (jnp.arange(top)[None, :] + turn) % top, axis=1)


def portions_of(count, total, bound, skew, full):
    portions = [(1 << 20) // math.isqrt(rank ** skew) + 1 for rank in range(1, count + 1)]
    largest = bound if full else min(bound, max(-(-total // count), total * portions[0] // sum(portions)))
    least = 1 if total - largest >= count - 1 else 0
    given, rest = [largest] + [least] * (count - 1), total - largest - least * (count - 1)
    while rest > 0:
        free = [i for i in range(1, count) if given[i] < largest] or [i for i in range(1, count) if given[i] < bound]
        whole, remaining = sum([portions[i] for i in free]), rest
        for i in free:
            addition = min(bound - given[i], max(1, remaining * portions[i] // whole), rest)
            given[i] = given[i] + addition
            rest = rest - addition
    return np.array(given)


def normal_values(key, extent, width, limit, split=(), kind=jnp.bfloat16):
    values = jax.random.normal(key, extent, jnp.float32) * width
    if len(split) > 0:
        values = levels(key, extent, split, -0.22, 0.18) * values
    return jnp.clip(values, min=-limit, max=limit).astype(kind)


def setup_inputs(seed: int = 0) -> dict:
    keys = jax.random.split(jax.random.key(seed), 15)
    patches = normal_values(keys[0], (VIS_ALL, D), 1.0, 6.0, ((0, 128),))
    vis_gain = jnp.clip(1.0 + 0.15 * jax.random.normal(keys[1], (D,), jnp.float32), 0.25, 1.75)
    vis_qkv = draw_vis_qkv(jax.random.fold_in(keys[14], 71), 0)
    vis_out = normal_values(keys[3], (D, D), D ** -0.5, 0.15625, ((0, 16),))
    merge_gain = jnp.clip(1.0 + 0.15 * jax.random.normal(keys[4], (D,), jnp.float32), 0.25, 1.75)
    merge_w = normal_values(keys[5], (MRG, D), MRG ** -0.5, 0.078125, ((0, 16),))
    image_blocks = jax.vmap(lambda own: ragged(own, IMGS, VT // 4, VT // 8, 2))(jax.random.split(keys[6], N_GRP)).reshape((N_GRP, IMGS)).astype(jnp.int32)
    dest_group_keys = jax.random.split(jax.random.fold_in(keys[7], 1), MTOT // MT)
    dest_group_turns = jax.random.permutation(jax.random.fold_in(keys[7], 3), MTOT // MT)
    dest_group = jax.vmap(lambda own, number: routed_block(jax.random.fold_in(keys[7], 2), own, number, MT, N_GRP, 1, CAP, 2))(dest_group_keys, dest_group_turns).reshape((MTOT, 1))
    slot_rows = jax.vmap(lambda own: jax.random.permutation(own, TXT_DEV))(jax.random.split(keys[8], N_GRP * N_SEQ)).reshape((N_GRP, N_SEQ, TXT_DEV)).astype(jnp.int32)
    prompt_len = touch_ends(jax.random.randint(keys[9], (N_GRP,), PT // 4, PT + 1), jax.random.fold_in(keys[9], 1), PT // 4, PT).astype(jnp.int32)
    text_emb = normal_values(keys[10], (TXT_ALL, D), 1.0, 6.0, ((0, 128),))
    txt_gain = jnp.clip(1.0 + 0.15 * jax.random.normal(keys[11], (D,), jnp.float32), 0.25, 1.75)
    txt_qkv = draw_txt_qkv(jax.random.fold_in(keys[14], 71), 0)
    txt_out = normal_values(keys[13], (D, D), D ** -0.5, 0.15625, ((0, 16),))
    return dict(patches=patches, vis_gain=vis_gain, vis_qkv=vis_qkv, vis_out=vis_out, merge_gain=merge_gain, merge_w=merge_w, image_blocks=image_blocks, dest_group=dest_group, slot_rows=slot_rows, prompt_len=prompt_len, text_emb=text_emb, txt_gain=txt_gain, txt_qkv=txt_qkv, txt_out=txt_out)


def layer_norm(row_block, scale_gain):
    values_f = row_block.astype(jnp.float32)
    row_mean = lax.optimization_barrier(jnp.mean(values_f, axis=-1, keepdims=True))
    centred = values_f - row_mean
    variance = lax.optimization_barrier(jnp.mean(centred * centred, axis=-1, keepdims=True))
    return centred * lax.rsqrt(variance + 1e-06) * scale_gain

def rms_norm(row_block, scale_gain):
    values_f = row_block.astype(jnp.float32)
    return values_f * lax.rsqrt(lax.optimization_barrier(jnp.mean(values_f * values_f, axis=-1, keepdims=True)) + 1e-06) * scale_gain

def split_heads(array):
    return array.reshape(array.shape[0], HEADS, HEAD_DIM).transpose(1, 0, 2)

def attend(queries, key_rows, value_rows, allowed):

    def one_head(stacked):
        head_q, head_k, head_v = stacked
        scores = jnp.dot(head_q, head_k.T, preferred_element_type=jnp.float32) * HEAD_DIM ** (-0.5)
        scores = jnp.where(allowed, scores, -1e+30)
        row_max = lax.optimization_barrier(jnp.max(scores, axis=-1, keepdims=True))
        expo = jnp.exp(scores - row_max)
        probabilities = (expo / lax.optimization_barrier(jnp.sum(expo, axis=-1, keepdims=True))).astype(jnp.bfloat16)
        return jnp.dot(probabilities, head_v, preferred_element_type=jnp.float32).astype(jnp.bfloat16)
    joined = lax.map(one_head, (split_heads(queries), split_heads(key_rows), split_heads(value_rows)))
    return joined.transpose(1, 0, 2).reshape(queries.shape[0], HEADS * HEAD_DIM)

def reference(patches, vis_gain, vis_qkv, vis_out, merge_gain, merge_w, image_blocks, dest_group, slot_rows, prompt_len, text_emb, txt_gain, txt_qkv, txt_out):

    def vision_group(stacked):
        group_rows, blocks_row = stacked
        normed = layer_norm(group_rows, vis_gain).astype(jnp.bfloat16)
        queries = jnp.dot(normed, vis_qkv[0], preferred_element_type=jnp.float32).astype(jnp.bfloat16)
        key_rows = jnp.dot(normed, vis_qkv[1], preferred_element_type=jnp.float32).astype(jnp.bfloat16)
        value_rows = jnp.dot(normed, vis_qkv[2], preferred_element_type=jnp.float32).astype(jnp.bfloat16)
        bounds = jnp.cumsum(blocks_row).astype(jnp.int32)[:-1]
        merged_index = (jnp.arange(VT) // 4).astype(jnp.int32)
        segment_ids = lax.optimization_barrier(jnp.sum((merged_index[:, None] >= bounds[None, :]).astype(jnp.int32), axis=1))
        allowed = segment_ids[:, None] == segment_ids[None, :]
        heads_out = attend(queries, key_rows, value_rows, allowed)
        residual_sum = group_rows.astype(jnp.float32) + jnp.dot(heads_out, vis_out, preferred_element_type=jnp.float32)
        merged_in = layer_norm(residual_sum, merge_gain).astype(jnp.bfloat16).reshape(VT // 4, 4 * D)
        return jnp.dot(merged_in, merge_w, preferred_element_type=jnp.float32).astype(jnp.bfloat16)
    visual = lax.map(vision_group, (patches.reshape(N_GRP, VT, D), image_blocks)).reshape(MTOT, D)
    dest_rows = dest_group[:, 0].astype(jnp.int32).reshape(N_GRP * N_SEQ, MT)
    onehot = (dest_rows[:, :, None] == jnp.arange(N_GRP, dtype=jnp.int32)[None, None, :]).astype(jnp.int32)
    slot_rank = lax.optimization_barrier(jnp.sum((jnp.cumsum(onehot, axis=1).astype(jnp.int32) - 1) * onehot, axis=2)).astype(jnp.int32)
    device = jnp.arange(N_GRP * N_SEQ, dtype=jnp.int32)[:, None]
    src_grp = device // N_SEQ
    seq_idx = jnp.broadcast_to(device % N_SEQ, dest_rows.shape).astype(jnp.int32)
    slot_index = (src_grp * CAP + slot_rank).astype(jnp.int32)
    text_row = slot_rows[dest_rows, seq_idx, slot_index].astype(jnp.int32)
    target = ((dest_rows * N_SEQ + seq_idx) * TXT_DEV + text_row).astype(jnp.int32)
    hidden = text_emb.at[target.reshape(-1)].set(visual)

    def text_group(stacked):
        group_rows, length = stacked
        normed = rms_norm(group_rows, txt_gain).astype(jnp.bfloat16)
        queries = jnp.dot(normed, txt_qkv[0], preferred_element_type=jnp.float32).astype(jnp.bfloat16)
        key_rows = jnp.dot(normed, txt_qkv[1], preferred_element_type=jnp.float32).astype(jnp.bfloat16)
        value_rows = jnp.dot(normed, txt_qkv[2], preferred_element_type=jnp.float32).astype(jnp.bfloat16)
        positions = jnp.arange(PT, dtype=jnp.int32)
        allowed = (positions[None, :] <= positions[:, None]) & (positions[None, :] < length)
        heads_out = attend(queries, key_rows, value_rows, allowed)
        return group_rows.astype(jnp.float32) + jnp.dot(heads_out, txt_out, preferred_element_type=jnp.float32)
    text_out = lax.map(text_group, (hidden.reshape(N_GRP, PT, D), prompt_len))
    return text_out.reshape(TXT_ALL, D)
```

```python
import jax
import jax.numpy as jnp
from jax import lax
from jax.sharding import PartitionSpec as P

HEAD_DIM = 104


def layer_norm(row_block, scale_gain):
    values_f = row_block.astype(jnp.float32)
    row_mean = jnp.mean(values_f, axis=-1, keepdims=True)
    centred = values_f - row_mean
    variance = jnp.mean(centred * centred, axis=-1, keepdims=True)
    return centred * lax.rsqrt(variance + 1e-06) * scale_gain


def rms_norm(row_block, scale_gain):
    values_f = row_block.astype(jnp.float32)
    return (
        values_f
        * lax.rsqrt(jnp.mean(values_f * values_f, axis=-1, keepdims=True) + 1e-06)
        * scale_gain
    )


def projector(weights, shard_piece):
    return jnp.einsum(
        "rd,kde->kre", shard_piece, weights, preferred_element_type=jnp.float32
    ).astype(jnp.bfloat16)


def attend_local(queries, key_rows, value_rows, allowed_fn):
    length = queries.shape[0]
    head_width = queries.shape[1]
    head_count = head_width // HEAD_DIM
    block_rows = min(512, length)
    block_count = length // block_rows
    query_blocks = queries.reshape(block_count, block_rows, head_count, HEAD_DIM)
    key_heads = key_rows.reshape(length, head_count, HEAD_DIM)
    value_heads = value_rows.reshape(length, head_count, HEAD_DIM)

    def one_block(block_item):
        query_part, first_row = block_item
        scores = jnp.einsum(
            "qhe,khe->hqk", query_part, key_heads, preferred_element_type=jnp.float32
        ) * HEAD_DIM ** (-0.5)
        allowed = allowed_fn(first_row + jnp.arange(block_rows, dtype=jnp.int32))
        scores = jnp.where(allowed[None], scores, -1e30)
        row_max = jnp.max(scores, axis=-1, keepdims=True)
        expo = jnp.exp(scores - row_max)
        probabilities = (expo / jnp.sum(expo, axis=-1, keepdims=True)).astype(jnp.bfloat16)
        return jnp.einsum(
            "hqk,khe->qhe", probabilities, value_heads, preferred_element_type=jnp.float32
        ).astype(jnp.bfloat16)

    starts = jnp.arange(block_count, dtype=jnp.int32) * block_rows
    joined = lax.map(one_block, (query_blocks, starts))
    return joined.reshape(length, head_width)


def heads_to_rows(heads, seq_count):
    length, width = heads.shape
    rows = length // seq_count
    blocks = heads.reshape(seq_count, rows, width)
    swapped = lax.all_to_all(blocks, "seq", split_axis=0, concat_axis=0, tiled=True)
    return swapped.transpose(1, 0, 2).reshape(rows, seq_count * width)


def per_device(
    patches,
    vis_gain,
    vis_qkv,
    vis_out,
    merge_gain,
    merge_w,
    image_blocks,
    dest_group,
    slot_rows,
    prompt_len,
    text_emb,
    txt_gain,
    txt_qkv,
    txt_out,
):
    seq_count = lax.axis_size("seq")
    groups = lax.axis_size("grp")
    token_count = patches.shape[0]
    model_width = patches.shape[1]
    group_patches = token_count * seq_count
    vis_out_full = lax.all_gather(vis_out, "seq", axis=0, tiled=True)
    txt_out_full = lax.all_gather(txt_out, "seq", axis=0, tiled=True)
    vis_normed = layer_norm(patches, vis_gain).astype(jnp.bfloat16)
    vis_proj = projector(vis_qkv, lax.all_gather(vis_normed, "seq", axis=0, tiled=True))
    bounds = jnp.cumsum(image_blocks[0])[:-1]

    def segment(indices):
        return jnp.sum(((indices // 4)[:, None] >= bounds[None, :]).astype(jnp.int32), axis=1)

    key_segments = segment(jnp.arange(group_patches, dtype=jnp.int32))

    def vis_allowed(row_indices):
        return segment(row_indices)[:, None] == key_segments[None, :]

    vis_heads = attend_local(vis_proj[0], vis_proj[1], vis_proj[2], vis_allowed)
    vis_attn = jnp.dot(
        heads_to_rows(vis_heads, seq_count), vis_out_full, preferred_element_type=jnp.float32
    )
    residual_sum = patches.astype(jnp.float32) + vis_attn
    merged_in = (
        layer_norm(residual_sum, merge_gain)
        .astype(jnp.bfloat16)
        .reshape(token_count // 4, 4 * model_width)
    )
    feature_slices = lax.all_to_all(merged_in, "seq", split_axis=1, concat_axis=0, tiled=True)
    picked = feature_slices
    visual = lax.psum_scatter(
        jnp.dot(picked, merge_w, preferred_element_type=jnp.float32),
        "seq",
        scatter_dimension=0,
        tiled=True,
    ).astype(jnp.bfloat16)
    dest_rows = dest_group[:, 0]
    merged_rows = dest_rows.shape[0]
    capacity = max(2, 2 * merged_rows // groups)
    onehot = (dest_rows[:, None] == jnp.arange(groups, dtype=jnp.int32)[None, :]).astype(jnp.int32)
    slot_rank = jnp.sum((jnp.cumsum(onehot, axis=0) - 1) * onehot, axis=1)
    selector = (
        (dest_rows[None, None, :] == jnp.arange(groups, dtype=jnp.int32)[:, None, None])
        & (slot_rank[None, None, :] == jnp.arange(capacity, dtype=jnp.int32)[None, :, None])
    ).astype(jnp.bfloat16)
    outgoing = jnp.einsum(
        "gct,td->gcd", selector, visual, preferred_element_type=jnp.float32
    ).astype(jnp.bfloat16)
    arrived_flags = jnp.sum(selector.astype(jnp.float32), axis=2).astype(jnp.bfloat16)
    incoming, arrived = (
        lax.all_to_all(outgoing, "grp", split_axis=0, concat_axis=0, tiled=True),
        lax.all_to_all(arrived_flags, "grp", split_axis=0, concat_axis=0, tiled=True),
    )
    prompt_rows = text_emb.shape[0]
    slot_targets = slot_rows[0, 0, : groups * capacity]
    placement_map = (
        slot_targets[None, :] == jnp.arange(prompt_rows, dtype=jnp.int32)[:, None]
    ).astype(jnp.bfloat16)
    placement_map = placement_map * arrived.reshape(1, groups * capacity)
    replaced = jnp.sum(placement_map.astype(jnp.float32), axis=1, keepdims=True)
    placed = jnp.dot(
        placement_map,
        incoming.reshape(groups * capacity, model_width),
        preferred_element_type=jnp.float32,
    )
    hidden = (text_emb.astype(jnp.float32) * (1.0 - replaced) + placed).astype(jnp.bfloat16)
    txt_normed = rms_norm(hidden, txt_gain).astype(jnp.bfloat16)
    txt_proj = projector(txt_qkv, lax.all_gather(txt_normed, "seq", axis=0, tiled=True))
    length = prompt_len[0]
    key_positions = jnp.arange(prompt_rows * seq_count, dtype=jnp.int32)

    def txt_allowed(row_indices):
        return (key_positions[None, :] <= row_indices[:, None]) & (key_positions[None, :] < length)

    txt_heads = attend_local(txt_proj[0], txt_proj[1], txt_proj[2], txt_allowed)
    txt_attn = jnp.dot(
        heads_to_rows(txt_heads, seq_count), txt_out_full, preferred_element_type=jnp.float32
    )
    return hidden.astype(jnp.float32) + txt_attn


def solution(mesh):
    in_specs = (
        P(("grp", "seq"), None),
        P(),
        P(None, None, "seq"),
        P("seq", None),
        P(),
        P("seq", None),
        P("grp", None),
        P(("grp", "seq"), None),
        P("grp", "seq", None),
        P("grp"),
        P(("grp", "seq"), None),
        P(),
        P(None, None, "seq"),
        P("seq", None),
    )
    out_specs = P(("grp", "seq"), None)
    return jax.shard_map(
        per_device, mesh=mesh, in_specs=in_specs, out_specs=out_specs, check_vma=False
    )
```

```python
import jax
import jax.numpy as jnp
from jax import lax
from jax.sharding import PartitionSpec as P

HEAD_DIM = 104


def layer_norm(row_block, scale_gain):
    values_f = row_block.astype(jnp.float32)
    row_mean = jnp.mean(values_f, axis=-1, keepdims=True)
    centred = values_f - row_mean
    variance = jnp.mean(centred * centred, axis=-1, keepdims=True)
    return centred * lax.rsqrt(variance + 1e-06) * scale_gain


def rms_norm(row_block, scale_gain):
    values_f = row_block.astype(jnp.float32)
    return (
        values_f
        * lax.rsqrt(jnp.mean(values_f * values_f, axis=-1, keepdims=True) + 1e-06)
        * scale_gain
    )


def projector(weights, shard_piece):
    return jnp.einsum(
        "rd,kde->kre", shard_piece, weights, preferred_element_type=jnp.float32
    ).astype(jnp.bfloat16)


def attend_local(queries, key_rows, value_rows, allowed_fn):
    length = queries.shape[0]
    head_width = queries.shape[1]
    head_count = head_width // HEAD_DIM
    block_rows = min(512, length)
    block_count = length // block_rows
    query_blocks = queries.reshape(block_count, block_rows, head_count, HEAD_DIM)
    key_heads = key_rows.reshape(length, head_count, HEAD_DIM)
    value_heads = value_rows.reshape(length, head_count, HEAD_DIM)

    def one_block(block_item):
        query_part, first_row = block_item
        scores = jnp.einsum(
            "qhe,khe->hqk", query_part, key_heads, preferred_element_type=jnp.float32
        ) * HEAD_DIM ** (-0.5)
        allowed = allowed_fn(first_row + jnp.arange(block_rows, dtype=jnp.int32))
        scores = jnp.where(allowed[None], scores, -1e30)
        row_max = jnp.max(scores, axis=-1, keepdims=True)
        expo = jnp.exp(scores - row_max)
        probabilities = (expo / jnp.sum(expo, axis=-1, keepdims=True)).astype(jnp.bfloat16)
        return jnp.einsum(
            "hqk,khe->qhe", probabilities, value_heads, preferred_element_type=jnp.float32
        ).astype(jnp.bfloat16)

    starts = jnp.arange(block_count, dtype=jnp.int32) * block_rows
    joined = lax.map(one_block, (query_blocks, starts))
    return joined.reshape(length, head_width)


def heads_to_rows(heads, seq_count):
    length, width = heads.shape
    rows = length // seq_count
    blocks = heads.reshape(seq_count, rows, width)
    swapped = lax.all_to_all(blocks, "seq", split_axis=0, concat_axis=0, tiled=True)
    return swapped.transpose(1, 0, 2).reshape(rows, seq_count * width)


def gather_shared(w_local):
    half = w_local.shape[1] // 2
    groups = lax.axis_size("grp")
    core = lax.axis_index("grp") % 2
    mine = lax.dynamic_slice_in_dim(w_local, core * half, half, axis=1)
    mine_full = lax.all_gather(mine, "seq", axis=0, tiled=True)
    other_full = lax.ppermute(mine_full, "grp", [(g, g ^ 1) for g in range(groups)])
    return mine_full, other_full, core


def project_shared(rows, shared):
    mine_full, other_full, core = shared
    out_mine = jnp.dot(rows, mine_full, preferred_element_type=jnp.float32)
    out_other = jnp.dot(rows, other_full, preferred_element_type=jnp.float32)
    first = jnp.where(core == 0, out_mine, out_other)
    second = jnp.where(core == 0, out_other, out_mine)
    return jnp.concatenate([first, second], axis=1)


def per_device(
    patches,
    vis_gain,
    vis_qkv,
    vis_out,
    merge_gain,
    merge_w,
    image_blocks,
    dest_group,
    slot_rows,
    prompt_len,
    text_emb,
    txt_gain,
    txt_qkv,
    txt_out,
):
    seq_count = lax.axis_size("seq")
    groups = lax.axis_size("grp")
    token_count = patches.shape[0]
    model_width = patches.shape[1]
    group_patches = token_count * seq_count
    vis_normed = layer_norm(patches, vis_gain).astype(jnp.bfloat16)
    vis_gathered = lax.all_gather(vis_normed, "seq", axis=0, tiled=True)
    vis_gathered, vis_out, txt_out = lax.optimization_barrier((vis_gathered, vis_out, txt_out))
    vis_out_full = gather_shared(vis_out)
    vis_proj = projector(vis_qkv, vis_gathered)
    bounds = jnp.cumsum(image_blocks[0])[:-1]

    def segment(indices):
        return jnp.sum(((indices // 4)[:, None] >= bounds[None, :]).astype(jnp.int32), axis=1)

    key_segments = segment(jnp.arange(group_patches, dtype=jnp.int32))

    def vis_allowed(row_indices):
        return segment(row_indices)[:, None] == key_segments[None, :]

    vis_heads = attend_local(vis_proj[0], vis_proj[1], vis_proj[2], vis_allowed)
    vis_heads, txt_out = lax.optimization_barrier((vis_heads, txt_out))
    txt_out_full = gather_shared(txt_out)
    vis_attn = project_shared(heads_to_rows(vis_heads, seq_count), vis_out_full)
    residual_sum = patches.astype(jnp.float32) + vis_attn
    merged_in = (
        layer_norm(residual_sum, merge_gain)
        .astype(jnp.bfloat16)
        .reshape(token_count // 4, 4 * model_width)
    )
    feature_slices = lax.all_to_all(merged_in, "seq", split_axis=1, concat_axis=0, tiled=True)
    merge_partial = jnp.dot(feature_slices, merge_w, preferred_element_type=jnp.float32)
    merge_partial = lax.optimization_barrier((merge_partial, txt_out_full[0]))[0]
    visual = lax.psum_scatter(
        merge_partial,
        "seq",
        scatter_dimension=0,
        tiled=True,
    ).astype(jnp.bfloat16)
    dest_rows = dest_group[:, 0]
    merged_rows = dest_rows.shape[0]
    capacity = max(2, 2 * merged_rows // groups)
    onehot = (dest_rows[:, None] == jnp.arange(groups, dtype=jnp.int32)[None, :]).astype(jnp.int32)
    slot_rank = jnp.sum((jnp.cumsum(onehot, axis=0) - 1) * onehot, axis=1)
    selector = (
        (dest_rows[None, None, :] == jnp.arange(groups, dtype=jnp.int32)[:, None, None])
        & (slot_rank[None, None, :] == jnp.arange(capacity, dtype=jnp.int32)[None, :, None])
    ).astype(jnp.bfloat16)
    outgoing = jnp.einsum(
        "gct,td->gcd", selector, visual, preferred_element_type=jnp.float32
    ).astype(jnp.bfloat16)
    arrived_flags = jnp.sum(selector.astype(jnp.float32), axis=2).astype(jnp.bfloat16)
    flag_row = jnp.pad(arrived_flags, ((0, 0), (0, model_width - capacity)))[:, None, :]
    payload = lax.all_to_all(
        jnp.concatenate([outgoing, flag_row], axis=1), "grp", split_axis=0, concat_axis=0, tiled=True
    )
    incoming = payload[:, :capacity, :]
    arrived = payload[:, capacity, :capacity]
    prompt_rows = text_emb.shape[0]
    slot_targets = slot_rows[0, 0, : groups * capacity]
    placement_map = (
        slot_targets[None, :] == jnp.arange(prompt_rows, dtype=jnp.int32)[:, None]
    ).astype(jnp.bfloat16)
    placement_map = placement_map * arrived.reshape(1, groups * capacity)
    replaced = jnp.sum(placement_map.astype(jnp.float32), axis=1, keepdims=True)
    placed = jnp.dot(
        placement_map,
        incoming.reshape(groups * capacity, model_width),
        preferred_element_type=jnp.float32,
    )
    hidden = (text_emb.astype(jnp.float32) * (1.0 - replaced) + placed).astype(jnp.bfloat16)
    txt_normed = rms_norm(hidden, txt_gain).astype(jnp.bfloat16)
    txt_proj = projector(txt_qkv, lax.all_gather(txt_normed, "seq", axis=0, tiled=True))
    length = prompt_len[0]
    key_positions = jnp.arange(prompt_rows * seq_count, dtype=jnp.int32)

    def txt_allowed(row_indices):
        return (key_positions[None, :] <= row_indices[:, None]) & (key_positions[None, :] < length)

    txt_heads = attend_local(txt_proj[0], txt_proj[1], txt_proj[2], txt_allowed)
    txt_attn = project_shared(heads_to_rows(txt_heads, seq_count), txt_out_full)
    return hidden.astype(jnp.float32) + txt_attn


def solution(mesh):
    in_specs = (
        P(("grp", "seq"), None),
        P(),
        P(None, None, "seq"),
        P("seq", None),
        P(),
        P("seq", None),
        P("grp", None),
        P(("grp", "seq"), None),
        P("grp", "seq", None),
        P("grp"),
        P(("grp", "seq"), None),
        P(),
        P(None, None, "seq"),
        P("seq", None),
    )
    out_specs = P(("grp", "seq"), None)
    return jax.shard_map(
        per_device, mesh=mesh, in_specs=in_specs, out_specs=out_specs, check_vma=False
    )
```

```python
import functools

import jax
import jax.numpy as jnp
from jax import lax
from jax.sharding import PartitionSpec as P

HEAD_DIM = 104


def layer_norm(row_block, scale_gain):
    values_f = row_block.astype(jnp.float32)
    row_mean = jnp.mean(values_f, axis=-1, keepdims=True)
    centred = values_f - row_mean
    variance = jnp.mean(centred * centred, axis=-1, keepdims=True)
    return centred * lax.rsqrt(variance + 1e-06) * scale_gain


def rms_norm(row_block, scale_gain):
    values_f = row_block.astype(jnp.float32)
    return (
        values_f
        * lax.rsqrt(jnp.mean(values_f * values_f, axis=-1, keepdims=True) + 1e-06)
        * scale_gain
    )


def projector(weights, shard_piece):
    return jnp.einsum(
        "rd,kde->kre", shard_piece, weights, preferred_element_type=jnp.float32
    ).astype(jnp.bfloat16)


def attend_local(queries, key_rows, value_rows, allowed_fn):
    length = queries.shape[0]
    head_width = queries.shape[1]
    head_count = head_width // HEAD_DIM
    block_rows = min(512, length)
    block_count = length // block_rows
    query_blocks = queries.reshape(block_count, block_rows, head_count, HEAD_DIM)
    key_heads = key_rows.reshape(length, head_count, HEAD_DIM)
    value_heads = value_rows.reshape(length, head_count, HEAD_DIM)

    def one_block(block_item):
        query_part, first_row = block_item
        scores = jnp.einsum(
            "qhe,khe->hqk", query_part, key_heads, preferred_element_type=jnp.float32
        ) * HEAD_DIM ** (-0.5)
        allowed = allowed_fn(first_row + jnp.arange(block_rows, dtype=jnp.int32))
        scores = jnp.where(allowed[None], scores, -1e30)
        row_max = jnp.max(scores, axis=-1, keepdims=True)
        expo = jnp.exp(scores - row_max)
        probabilities = (expo / jnp.sum(expo, axis=-1, keepdims=True)).astype(jnp.bfloat16)
        return jnp.einsum(
            "hqk,khe->qhe", probabilities, value_heads, preferred_element_type=jnp.float32
        ).astype(jnp.bfloat16)

    starts = jnp.arange(block_count, dtype=jnp.int32) * block_rows
    joined = lax.map(one_block, (query_blocks, starts))
    return joined.reshape(length, head_width)


def heads_to_rows(heads, seq_count):
    length, width = heads.shape
    rows = length // seq_count
    blocks = heads.reshape(seq_count, rows, width)
    swapped = lax.all_to_all(blocks, "seq", split_axis=0, concat_axis=0, tiled=True)
    return swapped.transpose(1, 0, 2).reshape(rows, seq_count * width)


def permute_gather_seq(piece, grid):
    ny, nx = grid
    seq_index = lax.axis_index("seq")
    y, x = seq_index // nx, seq_index % nx

    def shift(dy, dx):
        return [
            (a * nx + b, ((a + dy) % ny) * nx + (b + dx) % nx)
            for a in range(ny)
            for b in range(nx)
        ]

    row = jnp.stack([piece] + [lax.ppermute(piece, "seq", shift(0, dx)) for dx in range(1, nx)])
    full = jnp.stack([row] + [lax.ppermute(row, "seq", shift(dy, 0)) for dy in range(1, ny)])
    full = jnp.take(full, (y - jnp.arange(ny)) % ny, axis=0)
    full = jnp.take(full, (x - jnp.arange(nx)) % nx, axis=1)
    return full.reshape(ny * nx * piece.shape[0], piece.shape[1])


def gather_shared(w_local, grid):
    half = w_local.shape[1] // 2
    groups = lax.axis_size("grp")
    core = lax.axis_index("grp") % 2
    mine = lax.dynamic_slice_in_dim(w_local, core * half, half, axis=1)
    mine_full = permute_gather_seq(mine, grid)
    other_full = lax.ppermute(mine_full, "grp", [(g, g ^ 1) for g in range(groups)])
    return mine_full, other_full, core


def project_shared(rows, shared):
    mine_full, other_full, core = shared
    out_mine = jnp.dot(rows, mine_full, preferred_element_type=jnp.float32)
    out_other = jnp.dot(rows, other_full, preferred_element_type=jnp.float32)
    first = jnp.where(core == 0, out_mine, out_other)
    second = jnp.where(core == 0, out_other, out_mine)
    return jnp.concatenate([first, second], axis=1)


def per_device(
    grid,
    patches,
    vis_gain,
    vis_qkv,
    vis_out,
    merge_gain,
    merge_w,
    image_blocks,
    dest_group,
    slot_rows,
    prompt_len,
    text_emb,
    txt_gain,
    txt_qkv,
    txt_out,
):
    seq_count = lax.axis_size("seq")
    groups = lax.axis_size("grp")
    token_count = patches.shape[0]
    model_width = patches.shape[1]
    group_patches = token_count * seq_count
    vis_normed = layer_norm(patches, vis_gain).astype(jnp.bfloat16)
    vis_gathered = lax.all_gather(vis_normed, "seq", axis=0, tiled=True)
    vis_out_full = gather_shared(vis_out, grid)
    txt_out_full = gather_shared(txt_out, grid)
    vis_proj = projector(vis_qkv, vis_gathered)
    bounds = jnp.cumsum(image_blocks[0])[:-1]

    def segment(indices):
        return jnp.sum(((indices // 4)[:, None] >= bounds[None, :]).astype(jnp.int32), axis=1)

    key_segments = segment(jnp.arange(group_patches, dtype=jnp.int32))

    def vis_allowed(row_indices):
        return segment(row_indices)[:, None] == key_segments[None, :]

    vis_heads = attend_local(vis_proj[0], vis_proj[1], vis_proj[2], vis_allowed)
    vis_attn = project_shared(heads_to_rows(vis_heads, seq_count), vis_out_full)
    residual_sum = patches.astype(jnp.float32) + vis_attn
    merged_in = (
        layer_norm(residual_sum, merge_gain)
        .astype(jnp.bfloat16)
        .reshape(token_count // 4, 4 * model_width)
    )
    feature_slices = lax.all_to_all(merged_in, "seq", split_axis=1, concat_axis=0, tiled=True)
    merge_partial = jnp.dot(feature_slices, merge_w, preferred_element_type=jnp.float32)
    visual = lax.psum_scatter(
        merge_partial,
        "seq",
        scatter_dimension=0,
        tiled=True,
    ).astype(jnp.bfloat16)
    dest_rows = dest_group[:, 0]
    merged_rows = dest_rows.shape[0]
    capacity = max(2, 2 * merged_rows // groups)
    onehot = (dest_rows[:, None] == jnp.arange(groups, dtype=jnp.int32)[None, :]).astype(jnp.int32)
    slot_rank = jnp.sum((jnp.cumsum(onehot, axis=0) - 1) * onehot, axis=1)
    selector = (
        (dest_rows[None, None, :] == jnp.arange(groups, dtype=jnp.int32)[:, None, None])
        & (slot_rank[None, None, :] == jnp.arange(capacity, dtype=jnp.int32)[None, :, None])
    ).astype(jnp.bfloat16)
    outgoing = jnp.einsum(
        "gct,td->gcd", selector, visual, preferred_element_type=jnp.float32
    ).astype(jnp.bfloat16)
    arrived_flags = jnp.sum(selector.astype(jnp.float32), axis=2).astype(jnp.bfloat16)
    flag_row = jnp.pad(arrived_flags, ((0, 0), (0, model_width - capacity)))[:, None, :]
    payload = lax.all_to_all(
        jnp.concatenate([outgoing, flag_row], axis=1), "grp", split_axis=0, concat_axis=0, tiled=True
    )
    incoming = payload[:, :capacity, :]
    arrived = payload[:, capacity, :capacity]
    prompt_rows = text_emb.shape[0]
    slot_targets = slot_rows[0, 0, : groups * capacity]
    placement_map = (
        slot_targets[None, :] == jnp.arange(prompt_rows, dtype=jnp.int32)[:, None]
    ).astype(jnp.bfloat16)
    placement_map = placement_map * arrived.reshape(1, groups * capacity)
    replaced = jnp.sum(placement_map.astype(jnp.float32), axis=1, keepdims=True)
    placed = jnp.dot(
        placement_map,
        incoming.reshape(groups * capacity, model_width),
        preferred_element_type=jnp.float32,
    )
    hidden = (text_emb.astype(jnp.float32) * (1.0 - replaced) + placed).astype(jnp.bfloat16)
    txt_normed = rms_norm(hidden, txt_gain).astype(jnp.bfloat16)
    txt_proj = projector(txt_qkv, lax.all_gather(txt_normed, "seq", axis=0, tiled=True))
    length = prompt_len[0]
    key_positions = jnp.arange(prompt_rows * seq_count, dtype=jnp.int32)

    def txt_allowed(row_indices):
        return (key_positions[None, :] <= row_indices[:, None]) & (key_positions[None, :] < length)

    txt_heads = attend_local(txt_proj[0], txt_proj[1], txt_proj[2], txt_allowed)
    txt_attn = project_shared(heads_to_rows(txt_heads, seq_count), txt_out_full)
    return hidden.astype(jnp.float32) + txt_attn


def seq_grid(mesh):
    count = mesh.shape["seq"]
    try:
        xs = {d.coords[0] for d in mesh.devices.reshape(count, -1)[:, 0]}
        nx = len(xs)
    except Exception:
        nx = 1
    if nx <= 1 or count % nx:
        nx = max(d for d in range(1, count + 1) if count % d == 0 and d * d <= count)
    return count // nx, nx


def solution(mesh):
    in_specs = (
        P(("grp", "seq"), None),
        P(),
        P(None, None, "seq"),
        P("seq", None),
        P(),
        P("seq", None),
        P("grp", None),
        P(("grp", "seq"), None),
        P("grp", "seq", None),
        P("grp"),
        P(("grp", "seq"), None),
        P(),
        P(None, None, "seq"),
        P("seq", None),
    )
    out_specs = P(("grp", "seq"), None)
    return jax.shard_map(
        functools.partial(per_device, seq_grid(mesh)), mesh=mesh, in_specs=in_specs, out_specs=out_specs, check_vma=False
    )
```

```python
import jax
import jax.numpy as jnp
from jax import lax
from jax.sharding import PartitionSpec as P

HEAD_DIM = 104


def layer_norm(row_block, scale_gain):
    values_f = row_block.astype(jnp.float32)
    row_mean = jnp.mean(values_f, axis=-1, keepdims=True)
    centred = values_f - row_mean
    variance = jnp.mean(centred * centred, axis=-1, keepdims=True)
    return centred * lax.rsqrt(variance + 1e-06) * scale_gain


def rms_norm(row_block, scale_gain):
    values_f = row_block.astype(jnp.float32)
    return (
        values_f
        * lax.rsqrt(jnp.mean(values_f * values_f, axis=-1, keepdims=True) + 1e-06)
        * scale_gain
    )


def projector(weights, shard_piece):
    return jnp.einsum(
        "rd,kde->kre", shard_piece, weights, preferred_element_type=jnp.float32
    ).astype(jnp.bfloat16)


def attend_local(queries, key_rows, value_rows, allowed_fn):
    length = queries.shape[0]
    head_width = queries.shape[1]
    head_count = head_width // HEAD_DIM
    block_rows = min(512, length)
    block_count = length // block_rows
    query_blocks = queries.reshape(block_count, block_rows, head_count, HEAD_DIM)
    key_heads = key_rows.reshape(length, head_count, HEAD_DIM)
    value_heads = value_rows.reshape(length, head_count, HEAD_DIM)

    def one_block(block_item):
        query_part, first_row = block_item
        scores = jnp.einsum(
            "qhe,khe->hqk", query_part, key_heads, preferred_element_type=jnp.float32
        ) * HEAD_DIM ** (-0.5)
        allowed = allowed_fn(first_row + jnp.arange(block_rows, dtype=jnp.int32))
        scores = jnp.where(allowed[None], scores, -1e30)
        row_max = jnp.max(scores, axis=-1, keepdims=True)
        expo = jnp.exp(scores - row_max)
        probabilities = (expo / jnp.sum(expo, axis=-1, keepdims=True)).astype(jnp.bfloat16)
        return jnp.einsum(
            "hqk,khe->qhe", probabilities, value_heads, preferred_element_type=jnp.float32
        ).astype(jnp.bfloat16)

    starts = jnp.arange(block_count, dtype=jnp.int32) * block_rows
    joined = lax.map(one_block, (query_blocks, starts))
    return joined.reshape(length, head_width)


def heads_to_rows(heads, seq_count):
    length, width = heads.shape
    rows = length // seq_count
    blocks = heads.reshape(seq_count, rows, width)
    swapped = lax.all_to_all(blocks, "seq", split_axis=0, concat_axis=0, tiled=True)
    return swapped.transpose(1, 0, 2).reshape(rows, seq_count * width)


def per_device(
    patches,
    vis_gain,
    vis_qkv,
    vis_out,
    merge_gain,
    merge_w,
    image_blocks,
    dest_group,
    slot_rows,
    prompt_len,
    text_emb,
    txt_gain,
    txt_qkv,
    txt_out,
):
    seq_count = lax.axis_size("seq")
    groups = lax.axis_size("grp")
    token_count = patches.shape[0]
    model_width = patches.shape[1]
    group_patches = token_count * seq_count
    vis_normed = layer_norm(patches, vis_gain).astype(jnp.bfloat16)
    weight_rows = vis_out.shape[0]
    padded_rows = -(-weight_rows // 16) * 16
    pad = ((0, padded_rows - weight_rows), (0, 0))
    bundle = jnp.concatenate([vis_normed, jnp.pad(vis_out, pad), jnp.pad(txt_out, pad)], axis=0)
    bundle = lax.all_gather(bundle, "seq", axis=0, tiled=False)
    vis_gathered = bundle[:, :token_count].reshape(group_patches, model_width)
    vis_out_full = bundle[:, token_count : token_count + weight_rows].reshape(-1, model_width)
    txt_out_full = bundle[:, token_count + padded_rows : token_count + padded_rows + weight_rows].reshape(
        -1, model_width
    )
    vis_proj = projector(vis_qkv, vis_gathered)
    bounds = jnp.cumsum(image_blocks[0])[:-1]

    def segment(indices):
        return jnp.sum(((indices // 4)[:, None] >= bounds[None, :]).astype(jnp.int32), axis=1)

    key_segments = segment(jnp.arange(group_patches, dtype=jnp.int32))

    def vis_allowed(row_indices):
        return segment(row_indices)[:, None] == key_segments[None, :]

    vis_heads = attend_local(vis_proj[0], vis_proj[1], vis_proj[2], vis_allowed)
    vis_attn = jnp.dot(
        heads_to_rows(vis_heads, seq_count), vis_out_full, preferred_element_type=jnp.float32
    )
    residual_sum = patches.astype(jnp.float32) + vis_attn
    merged_in = (
        layer_norm(residual_sum, merge_gain)
        .astype(jnp.bfloat16)
        .reshape(token_count // 4, 4 * model_width)
    )
    feature_slices = lax.all_to_all(merged_in, "seq", split_axis=1, concat_axis=0, tiled=True)
    picked = feature_slices
    visual = lax.psum_scatter(
        jnp.dot(picked, merge_w, preferred_element_type=jnp.float32),
        "seq",
        scatter_dimension=0,
        tiled=True,
    ).astype(jnp.bfloat16)
    dest_rows = dest_group[:, 0]
    merged_rows = dest_rows.shape[0]
    capacity = max(2, 2 * merged_rows // groups)
    onehot = (dest_rows[:, None] == jnp.arange(groups, dtype=jnp.int32)[None, :]).astype(jnp.int32)
    slot_rank = jnp.sum((jnp.cumsum(onehot, axis=0) - 1) * onehot, axis=1)
    selector = (
        (dest_rows[None, None, :] == jnp.arange(groups, dtype=jnp.int32)[:, None, None])
        & (slot_rank[None, None, :] == jnp.arange(capacity, dtype=jnp.int32)[None, :, None])
    ).astype(jnp.bfloat16)
    outgoing = jnp.einsum(
        "gct,td->gcd", selector, visual, preferred_element_type=jnp.float32
    ).astype(jnp.bfloat16)
    arrived_flags = jnp.sum(selector.astype(jnp.float32), axis=2).astype(jnp.bfloat16)
    flag_row = jnp.pad(arrived_flags, ((0, 0), (0, model_width - capacity)))[:, None, :]
    payload = lax.all_to_all(
        jnp.concatenate([outgoing, flag_row], axis=1), "grp", split_axis=0, concat_axis=0, tiled=True
    )
    incoming = payload[:, :capacity, :]
    arrived = payload[:, capacity, :capacity]
    prompt_rows = text_emb.shape[0]
    slot_targets = slot_rows[0, 0, : groups * capacity]
    placement_map = (
        slot_targets[None, :] == jnp.arange(prompt_rows, dtype=jnp.int32)[:, None]
    ).astype(jnp.bfloat16)
    placement_map = placement_map * arrived.reshape(1, groups * capacity)
    replaced = jnp.sum(placement_map.astype(jnp.float32), axis=1, keepdims=True)
    placed = jnp.dot(
        placement_map,
        incoming.reshape(groups * capacity, model_width),
        preferred_element_type=jnp.float32,
    )
    hidden = (text_emb.astype(jnp.float32) * (1.0 - replaced) + placed).astype(jnp.bfloat16)
    txt_normed = rms_norm(hidden, txt_gain).astype(jnp.bfloat16)
    txt_proj = projector(txt_qkv, lax.all_gather(txt_normed, "seq", axis=0, tiled=True))
    length = prompt_len[0]
    key_positions = jnp.arange(prompt_rows * seq_count, dtype=jnp.int32)

    def txt_allowed(row_indices):
        return (key_positions[None, :] <= row_indices[:, None]) & (key_positions[None, :] < length)

    txt_heads = attend_local(txt_proj[0], txt_proj[1], txt_proj[2], txt_allowed)
    txt_attn = jnp.dot(
        heads_to_rows(txt_heads, seq_count), txt_out_full, preferred_element_type=jnp.float32
    )
    return hidden.astype(jnp.float32) + txt_attn


def solution(mesh):
    in_specs = (
        P(("grp", "seq"), None),
        P(),
        P(None, None, "seq"),
        P("seq", None),
        P(),
        P("seq", None),
        P("grp", None),
        P(("grp", "seq"), None),
        P("grp", "seq", None),
        P("grp"),
        P(("grp", "seq"), None),
        P(),
        P(None, None, "seq"),
        P("seq", None),
    )
    out_specs = P(("grp", "seq"), None)
    return jax.shard_map(
        per_device, mesh=mesh, in_specs=in_specs, out_specs=out_specs, check_vma=False
    )
```

```python
import jax
import jax.numpy as jnp
from jax import lax
from jax.sharding import PartitionSpec as P

HEAD_DIM = 104


def layer_norm(row_block, scale_gain):
    values_f = row_block.astype(jnp.float32)
    row_mean = jnp.mean(values_f, axis=-1, keepdims=True)
    centred = values_f - row_mean
    variance = jnp.mean(centred * centred, axis=-1, keepdims=True)
    return centred * lax.rsqrt(variance + 1e-06) * scale_gain


def rms_norm(row_block, scale_gain):
    values_f = row_block.astype(jnp.float32)
    return (
        values_f
        * lax.rsqrt(jnp.mean(values_f * values_f, axis=-1, keepdims=True) + 1e-06)
        * scale_gain
    )


def projector(weights, shard_piece):
    return jnp.einsum(
        "rd,kde->kre", shard_piece, weights, preferred_element_type=jnp.float32
    ).astype(jnp.bfloat16)


def attend_local(queries, key_rows, value_rows, allowed_fn):
    length = queries.shape[0]
    head_width = queries.shape[1]
    head_count = head_width // HEAD_DIM
    block_rows = min(512, length)
    block_count = length // block_rows
    query_blocks = queries.reshape(block_count, block_rows, head_count, HEAD_DIM)
    key_heads = key_rows.reshape(length, head_count, HEAD_DIM)
    value_heads = value_rows.reshape(length, head_count, HEAD_DIM)

    def one_block(block_item):
        query_part, first_row = block_item
        scores = jnp.einsum(
            "qhe,khe->hqk", query_part, key_heads, preferred_element_type=jnp.float32
        ) * HEAD_DIM ** (-0.5)
        allowed = allowed_fn(first_row + jnp.arange(block_rows, dtype=jnp.int32))
        scores = jnp.where(allowed[None], scores, -1e30)
        row_max = jnp.max(scores, axis=-1, keepdims=True)
        expo = jnp.exp(scores - row_max)
        probabilities = (expo / jnp.sum(expo, axis=-1, keepdims=True)).astype(jnp.bfloat16)
        return jnp.einsum(
            "hqk,khe->qhe", probabilities, value_heads, preferred_element_type=jnp.float32
        ).astype(jnp.bfloat16)

    starts = jnp.arange(block_count, dtype=jnp.int32) * block_rows
    joined = lax.map(one_block, (query_blocks, starts))
    return joined.reshape(length, head_width)


def heads_to_rows(heads, seq_count):
    length, width = heads.shape
    rows = length // seq_count
    blocks = heads.reshape(seq_count, rows, width)
    swapped = lax.all_to_all(blocks, "seq", split_axis=0, concat_axis=0, tiled=True)
    return swapped.transpose(1, 0, 2).reshape(rows, seq_count * width)


def per_device(
    patches,
    vis_gain,
    vis_qkv,
    vis_out,
    merge_gain,
    merge_w,
    image_blocks,
    dest_group,
    slot_rows,
    prompt_len,
    text_emb,
    txt_gain,
    txt_qkv,
    txt_out,
):
    seq_count = lax.axis_size("seq")
    groups = lax.axis_size("grp")
    token_count = patches.shape[0]
    model_width = patches.shape[1]
    group_patches = token_count * seq_count
    vis_out_full = lax.all_gather(vis_out, "seq", axis=0, tiled=True)
    vis_normed = layer_norm(patches, vis_gain).astype(jnp.bfloat16)
    vis_proj = projector(vis_qkv, lax.all_gather(vis_normed, "seq", axis=0, tiled=True))
    bounds = jnp.cumsum(image_blocks[0])[:-1]

    def segment(indices):
        return jnp.sum(((indices // 4)[:, None] >= bounds[None, :]).astype(jnp.int32), axis=1)

    key_segments = segment(jnp.arange(group_patches, dtype=jnp.int32))

    def vis_allowed(row_indices):
        return segment(row_indices)[:, None] == key_segments[None, :]

    vis_heads = attend_local(vis_proj[0], vis_proj[1], vis_proj[2], vis_allowed)
    vis_heads, txt_out = lax.optimization_barrier((vis_heads, txt_out))
    txt_out_full = lax.all_gather(txt_out, "seq", axis=0, tiled=True)
    vis_attn = jnp.dot(
        heads_to_rows(vis_heads, seq_count), vis_out_full, preferred_element_type=jnp.float32
    )
    residual_sum = patches.astype(jnp.float32) + vis_attn
    merged_in = (
        layer_norm(residual_sum, merge_gain)
        .astype(jnp.bfloat16)
        .reshape(token_count // 4, 4 * model_width)
    )
    feature_slices = lax.all_to_all(merged_in, "seq", split_axis=1, concat_axis=0, tiled=True)
    merge_partial = jnp.dot(feature_slices, merge_w, preferred_element_type=jnp.float32)
    merge_parts = lax.all_to_all(
        merge_partial.reshape(seq_count, -1, model_width), "seq", split_axis=0, concat_axis=0, tiled=True
    )
    visual = jnp.sum(merge_parts, axis=0).astype(jnp.bfloat16)
    dest_rows = dest_group[:, 0]
    merged_rows = dest_rows.shape[0]
    capacity = max(2, 2 * merged_rows // groups)
    onehot = (dest_rows[:, None] == jnp.arange(groups, dtype=jnp.int32)[None, :]).astype(jnp.int32)
    slot_rank = jnp.sum((jnp.cumsum(onehot, axis=0) - 1) * onehot, axis=1)
    selector = (
        (dest_rows[None, None, :] == jnp.arange(groups, dtype=jnp.int32)[:, None, None])
        & (slot_rank[None, None, :] == jnp.arange(capacity, dtype=jnp.int32)[None, :, None])
    ).astype(jnp.bfloat16)
    outgoing = jnp.einsum(
        "gct,td->gcd", selector, visual, preferred_element_type=jnp.float32
    ).astype(jnp.bfloat16)
    arrived_flags = jnp.sum(selector.astype(jnp.float32), axis=2).astype(jnp.bfloat16)
    flag_row = jnp.pad(arrived_flags, ((0, 0), (0, model_width - capacity)))[:, None, :]
    payload = lax.all_to_all(
        jnp.concatenate([outgoing, flag_row], axis=1), "grp", split_axis=0, concat_axis=0, tiled=True
    )
    incoming = payload[:, :capacity, :]
    arrived = payload[:, capacity, :capacity]
    prompt_rows = text_emb.shape[0]
    slot_targets = slot_rows[0, 0, : groups * capacity]
    placement_map = (
        slot_targets[None, :] == jnp.arange(prompt_rows, dtype=jnp.int32)[:, None]
    ).astype(jnp.bfloat16)
    placement_map = placement_map * arrived.reshape(1, groups * capacity)
    replaced = jnp.sum(placement_map.astype(jnp.float32), axis=1, keepdims=True)
    placed = jnp.dot(
        placement_map,
        incoming.reshape(groups * capacity, model_width),
        preferred_element_type=jnp.float32,
    )
    hidden = (text_emb.astype(jnp.float32) * (1.0 - replaced) + placed).astype(jnp.bfloat16)
    txt_normed = rms_norm(hidden, txt_gain).astype(jnp.bfloat16)
    txt_normed, txt_out_full = lax.optimization_barrier((txt_normed, txt_out_full))
    txt_proj = projector(txt_qkv, lax.all_gather(txt_normed, "seq", axis=0, tiled=True))
    length = prompt_len[0]
    key_positions = jnp.arange(prompt_rows * seq_count, dtype=jnp.int32)

    def txt_allowed(row_indices):
        return (key_positions[None, :] <= row_indices[:, None]) & (key_positions[None, :] < length)

    txt_heads = attend_local(txt_proj[0], txt_proj[1], txt_proj[2], txt_allowed)
    txt_attn = jnp.dot(
        heads_to_rows(txt_heads, seq_count), txt_out_full, preferred_element_type=jnp.float32
    )
    return hidden.astype(jnp.float32) + txt_attn


def solution(mesh):
    in_specs = (
        P(("grp", "seq"), None),
        P(),
        P(None, None, "seq"),
        P("seq", None),
        P(),
        P("seq", None),
        P("grp", None),
        P(("grp", "seq"), None),
        P("grp", "seq", None),
        P("grp"),
        P(("grp", "seq"), None),
        P(),
        P(None, None, "seq"),
        P("seq", None),
    )
    out_specs = P(("grp", "seq"), None)
    return jax.shard_map(
        per_device, mesh=mesh, in_specs=in_specs, out_specs=out_specs, check_vma=False
    )
```

```python
import jax
import jax.numpy as jnp
from jax import lax
from jax.sharding import PartitionSpec as P

HEAD_DIM = 104


def layer_norm(row_block, scale_gain):
    values_f = row_block.astype(jnp.float32)
    row_mean = jnp.mean(values_f, axis=-1, keepdims=True)
    centred = values_f - row_mean
    variance = jnp.mean(centred * centred, axis=-1, keepdims=True)
    return centred * lax.rsqrt(variance + 1e-06) * scale_gain


def rms_norm(row_block, scale_gain):
    values_f = row_block.astype(jnp.float32)
    return (
        values_f
        * lax.rsqrt(jnp.mean(values_f * values_f, axis=-1, keepdims=True) + 1e-06)
        * scale_gain
    )


def projector(weights, shard_piece):
    return jnp.einsum(
        "rd,kde->kre", shard_piece, weights, preferred_element_type=jnp.float32
    ).astype(jnp.bfloat16)


def attend_local(queries, key_rows, value_rows, allowed_fn):
    length = queries.shape[0]
    head_width = queries.shape[1]
    head_count = head_width // HEAD_DIM
    block_rows = min(512, length)
    block_count = length // block_rows
    query_blocks = queries.reshape(block_count, block_rows, head_count, HEAD_DIM)
    key_heads = key_rows.reshape(length, head_count, HEAD_DIM)
    value_heads = value_rows.reshape(length, head_count, HEAD_DIM)

    def one_block(block_item):
        query_part, first_row = block_item
        scores = jnp.einsum(
            "qhe,khe->hqk", query_part, key_heads, preferred_element_type=jnp.float32
        ) * HEAD_DIM ** (-0.5)
        allowed = allowed_fn(first_row + jnp.arange(block_rows, dtype=jnp.int32))
        scores = jnp.where(allowed[None], scores, -1e30)
        row_max = jnp.max(scores, axis=-1, keepdims=True)
        expo = jnp.exp(scores - row_max)
        probabilities = (expo / jnp.sum(expo, axis=-1, keepdims=True)).astype(jnp.bfloat16)
        return jnp.einsum(
            "hqk,khe->qhe", probabilities, value_heads, preferred_element_type=jnp.float32
        ).astype(jnp.bfloat16)

    starts = jnp.arange(block_count, dtype=jnp.int32) * block_rows
    joined = lax.map(one_block, (query_blocks, starts))
    return joined.reshape(length, head_width)


def heads_to_rows(heads, seq_count):
    length, width = heads.shape
    rows = length // seq_count
    blocks = heads.reshape(seq_count, rows, width)
    swapped = lax.all_to_all(blocks, "seq", split_axis=0, concat_axis=0, tiled=True)
    return swapped.transpose(1, 0, 2).reshape(rows, seq_count * width)


def attend_causal(queries, key_rows, value_rows, allowed_fn):
    length = queries.shape[0]
    head_width = queries.shape[1]
    head_count = head_width // HEAD_DIM
    block_rows = min(512, length)
    block_count = length // block_rows
    key_heads = key_rows.reshape(length, head_count, HEAD_DIM)
    value_heads = value_rows.reshape(length, head_count, HEAD_DIM)
    outputs = []
    for block in range(block_count):
        first_row = block * block_rows
        key_end = first_row + block_rows
        query_part = queries[first_row:key_end].reshape(block_rows, head_count, HEAD_DIM)
        scores = jnp.einsum(
            "qhe,khe->hqk", query_part, key_heads[:key_end], preferred_element_type=jnp.float32
        ) * HEAD_DIM ** (-0.5)
        allowed = allowed_fn(first_row + jnp.arange(block_rows, dtype=jnp.int32))[:, :key_end]
        scores = jnp.where(allowed[None], scores, -1e30)
        row_max = jnp.max(scores, axis=-1, keepdims=True)
        expo = jnp.exp(scores - row_max)
        probabilities = (expo / jnp.sum(expo, axis=-1, keepdims=True)).astype(jnp.bfloat16)
        outputs.append(
            jnp.einsum(
                "hqk,khe->qhe", probabilities, value_heads[:key_end], preferred_element_type=jnp.float32
            ).astype(jnp.bfloat16)
        )
    return jnp.concatenate(outputs, axis=0).reshape(length, head_width)


def per_device(
    patches,
    vis_gain,
    vis_qkv,
    vis_out,
    merge_gain,
    merge_w,
    image_blocks,
    dest_group,
    slot_rows,
    prompt_len,
    text_emb,
    txt_gain,
    txt_qkv,
    txt_out,
):
    seq_count = lax.axis_size("seq")
    groups = lax.axis_size("grp")
    token_count = patches.shape[0]
    model_width = patches.shape[1]
    group_patches = token_count * seq_count
    vis_out_full = lax.all_gather(vis_out, "seq", axis=0, tiled=True)
    vis_normed = layer_norm(patches, vis_gain).astype(jnp.bfloat16)
    vis_proj = projector(vis_qkv, lax.all_gather(vis_normed, "seq", axis=0, tiled=True))
    bounds = jnp.cumsum(image_blocks[0])[:-1]

    def segment(indices):
        return jnp.sum(((indices // 4)[:, None] >= bounds[None, :]).astype(jnp.int32), axis=1)

    key_segments = segment(jnp.arange(group_patches, dtype=jnp.int32))

    def vis_allowed(row_indices):
        return segment(row_indices)[:, None] == key_segments[None, :]

    vis_heads = attend_local(vis_proj[0], vis_proj[1], vis_proj[2], vis_allowed)
    vis_heads, txt_out = lax.optimization_barrier((vis_heads, txt_out))
    txt_out_full = lax.all_gather(txt_out, "seq", axis=0, tiled=True)
    vis_attn = jnp.dot(
        heads_to_rows(vis_heads, seq_count), vis_out_full, preferred_element_type=jnp.float32
    )
    residual_sum = patches.astype(jnp.float32) + vis_attn
    merged_in = (
        layer_norm(residual_sum, merge_gain)
        .astype(jnp.bfloat16)
        .reshape(token_count // 4, 4 * model_width)
    )
    feature_slices = lax.all_to_all(merged_in, "seq", split_axis=1, concat_axis=0, tiled=True)
    merge_partial = jnp.dot(feature_slices, merge_w, preferred_element_type=jnp.float32)
    merge_parts = lax.all_to_all(
        merge_partial.astype(jnp.bfloat16).reshape(seq_count, -1, model_width),
        "seq",
        split_axis=0,
        concat_axis=0,
        tiled=True,
    )
    visual = jnp.sum(merge_parts.astype(jnp.float32), axis=0).astype(jnp.bfloat16)
    dest_rows = dest_group[:, 0]
    merged_rows = dest_rows.shape[0]
    capacity = max(2, 2 * merged_rows // groups)
    onehot = (dest_rows[:, None] == jnp.arange(groups, dtype=jnp.int32)[None, :]).astype(jnp.int32)
    slot_rank = jnp.sum((jnp.cumsum(onehot, axis=0) - 1) * onehot, axis=1)
    selector = (
        (dest_rows[None, None, :] == jnp.arange(groups, dtype=jnp.int32)[:, None, None])
        & (slot_rank[None, None, :] == jnp.arange(capacity, dtype=jnp.int32)[None, :, None])
    ).astype(jnp.bfloat16)
    outgoing = jnp.einsum(
        "gct,td->gcd", selector, visual, preferred_element_type=jnp.float32
    ).astype(jnp.bfloat16)
    arrived_flags = jnp.sum(selector.astype(jnp.float32), axis=2).astype(jnp.bfloat16)
    flag_row = jnp.pad(arrived_flags, ((0, 0), (0, model_width - capacity)))[:, None, :]
    payload = lax.all_to_all(
        jnp.concatenate([outgoing, flag_row], axis=1), "grp", split_axis=0, concat_axis=0, tiled=True
    )
    incoming = payload[:, :capacity, :]
    arrived = payload[:, capacity, :capacity]
    prompt_rows = text_emb.shape[0]
    slot_targets = slot_rows[0, 0, : groups * capacity]
    placement_map = (
        slot_targets[None, :] == jnp.arange(prompt_rows, dtype=jnp.int32)[:, None]
    ).astype(jnp.bfloat16)
    placement_map = placement_map * arrived.reshape(1, groups * capacity)
    replaced = jnp.sum(placement_map.astype(jnp.float32), axis=1, keepdims=True)
    placed = jnp.dot(
        placement_map,
        incoming.reshape(groups * capacity, model_width),
        preferred_element_type=jnp.float32,
    )
    hidden = (text_emb.astype(jnp.float32) * (1.0 - replaced) + placed).astype(jnp.bfloat16)
    txt_normed = rms_norm(hidden, txt_gain).astype(jnp.bfloat16)
    txt_normed, txt_out_full = lax.optimization_barrier((txt_normed, txt_out_full))
    txt_proj = projector(txt_qkv, lax.all_gather(txt_normed, "seq", axis=0, tiled=True))
    length = prompt_len[0]
    key_positions = jnp.arange(prompt_rows * seq_count, dtype=jnp.int32)

    def txt_allowed(row_indices):
        return (key_positions[None, :] <= row_indices[:, None]) & (key_positions[None, :] < length)

    txt_heads = attend_causal(txt_proj[0], txt_proj[1], txt_proj[2], txt_allowed)
    txt_attn = jnp.dot(
        heads_to_rows(txt_heads, seq_count), txt_out_full, preferred_element_type=jnp.float32
    )
    return hidden.astype(jnp.float32) + txt_attn


def solution(mesh):
    in_specs = (
        P(("grp", "seq"), None),
        P(),
        P(None, None, "seq"),
        P("seq", None),
        P(),
        P("seq", None),
        P("grp", None),
        P(("grp", "seq"), None),
        P("grp", "seq", None),
        P("grp"),
        P(("grp", "seq"), None),
        P(),
        P(None, None, "seq"),
        P("seq", None),
    )
    out_specs = P(("grp", "seq"), None)
    return jax.shard_map(
        per_device, mesh=mesh, in_specs=in_specs, out_specs=out_specs, check_vma=False
    )
```

```python
import jax
import jax.numpy as jnp
from jax import lax
from jax.sharding import PartitionSpec as P

HEAD_DIM = 104


def layer_norm(row_block, scale_gain):
    values_f = row_block.astype(jnp.float32)
    row_mean = jnp.mean(values_f, axis=-1, keepdims=True)
    centred = values_f - row_mean
    variance = jnp.mean(centred * centred, axis=-1, keepdims=True)
    return centred * lax.rsqrt(variance + 1e-06) * scale_gain


def rms_norm(row_block, scale_gain):
    values_f = row_block.astype(jnp.float32)
    return (
        values_f
        * lax.rsqrt(jnp.mean(values_f * values_f, axis=-1, keepdims=True) + 1e-06)
        * scale_gain
    )


def projector(weights, shard_piece):
    return jnp.einsum(
        "rd,kde->kre", shard_piece, weights, preferred_element_type=jnp.float32
    ).astype(jnp.bfloat16)


def attend_local(queries, key_rows, value_rows, allowed_fn):
    length = queries.shape[0]
    head_width = queries.shape[1]
    head_count = head_width // HEAD_DIM
    block_rows = min(512, length)
    block_count = length // block_rows
    query_blocks = queries.reshape(block_count, block_rows, head_count, HEAD_DIM)
    key_heads = key_rows.reshape(length, head_count, HEAD_DIM)
    value_heads = value_rows.reshape(length, head_count, HEAD_DIM)

    def one_block(block_item):
        query_part, first_row = block_item
        scores = jnp.einsum(
            "qhe,khe->hqk", query_part, key_heads, preferred_element_type=jnp.float32
        ) * HEAD_DIM ** (-0.5)
        allowed = allowed_fn(first_row + jnp.arange(block_rows, dtype=jnp.int32))
        scores = jnp.where(allowed[None], scores, -1e30)
        row_max = jnp.max(scores, axis=-1, keepdims=True)
        expo = jnp.exp(scores - row_max)
        probabilities = (expo / jnp.sum(expo, axis=-1, keepdims=True)).astype(jnp.bfloat16)
        return jnp.einsum(
            "hqk,khe->qhe", probabilities, value_heads, preferred_element_type=jnp.float32
        ).astype(jnp.bfloat16)

    starts = jnp.arange(block_count, dtype=jnp.int32) * block_rows
    joined = lax.map(one_block, (query_blocks, starts))
    return joined.reshape(length, head_width)


def heads_to_rows(heads, seq_count):
    length, width = heads.shape
    rows = length // seq_count
    blocks = heads.reshape(seq_count, rows, width)
    swapped = lax.all_to_all(blocks, "seq", split_axis=0, concat_axis=0, tiled=True)
    return swapped.transpose(1, 0, 2).reshape(rows, seq_count * width)


def attend_causal(queries, key_rows, value_rows, allowed_fn):
    length = queries.shape[0]
    head_width = queries.shape[1]
    head_count = head_width // HEAD_DIM
    block_rows = min(512, length)
    block_count = length // block_rows
    key_heads = key_rows.reshape(length, head_count, HEAD_DIM)
    value_heads = value_rows.reshape(length, head_count, HEAD_DIM)
    outputs = []
    for block in range(block_count):
        first_row = block * block_rows
        key_end = first_row + block_rows
        query_part = queries[first_row:key_end].reshape(block_rows, head_count, HEAD_DIM)
        scores = jnp.einsum(
            "qhe,khe->hqk", query_part, key_heads[:key_end], preferred_element_type=jnp.float32
        ) * HEAD_DIM ** (-0.5)
        allowed = allowed_fn(first_row + jnp.arange(block_rows, dtype=jnp.int32))[:, :key_end]
        scores = jnp.where(allowed[None], scores, -1e30)
        row_max = jnp.max(scores, axis=-1, keepdims=True)
        expo = jnp.exp(scores - row_max)
        probabilities = (expo / jnp.sum(expo, axis=-1, keepdims=True)).astype(jnp.bfloat16)
        outputs.append(
            jnp.einsum(
                "hqk,khe->qhe", probabilities, value_heads[:key_end], preferred_element_type=jnp.float32
            ).astype(jnp.bfloat16)
        )
    return jnp.concatenate(outputs, axis=0).reshape(length, head_width)


def core_half(w_local):
    half = w_local.shape[1] // 2
    core = lax.axis_index("grp") % 2
    return lax.dynamic_slice_in_dim(w_local, core * half, half, axis=1), core


def swap_cores(mine_full):
    groups = lax.axis_size("grp")
    return lax.ppermute(mine_full, "grp", [(g, g ^ 1) for g in range(groups)])


def project_halves(rows, mine_full, other_full, core):
    out_mine = jnp.dot(rows, mine_full, preferred_element_type=jnp.float32)
    out_other = jnp.dot(rows, other_full, preferred_element_type=jnp.float32)
    first = jnp.where(core == 0, out_mine, out_other)
    second = jnp.where(core == 0, out_other, out_mine)
    return jnp.concatenate([first, second], axis=1)


def per_device(
    patches,
    vis_gain,
    vis_qkv,
    vis_out,
    merge_gain,
    merge_w,
    image_blocks,
    dest_group,
    slot_rows,
    prompt_len,
    text_emb,
    txt_gain,
    txt_qkv,
    txt_out,
):
    seq_count = lax.axis_size("seq")
    groups = lax.axis_size("grp")
    token_count = patches.shape[0]
    model_width = patches.shape[1]
    group_patches = token_count * seq_count
    vis_normed = layer_norm(patches, vis_gain).astype(jnp.bfloat16)
    vis_mine, core = core_half(vis_out)
    weight_rows, half_width = vis_mine.shape
    packed_rows = weight_rows * half_width // model_width
    padded_rows = -(-packed_rows // 16) * 16
    packed = jnp.pad(vis_mine.reshape(packed_rows, model_width), ((0, padded_rows - packed_rows), (0, 0)))
    bundle = lax.all_gather(
        jnp.concatenate([vis_normed, packed], axis=0), "seq", axis=0, tiled=False
    )
    vis_gathered = bundle[:, :token_count].reshape(group_patches, model_width)
    vis_mine_full = bundle[:, token_count : token_count + packed_rows].reshape(
        seq_count * weight_rows, half_width
    )
    vis_other_full = swap_cores(vis_mine_full)
    vis_proj = projector(vis_qkv, vis_gathered)
    bounds = jnp.cumsum(image_blocks[0])[:-1]

    def segment(indices):
        return jnp.sum(((indices // 4)[:, None] >= bounds[None, :]).astype(jnp.int32), axis=1)

    key_segments = segment(jnp.arange(group_patches, dtype=jnp.int32))

    def vis_allowed(row_indices):
        return segment(row_indices)[:, None] == key_segments[None, :]

    vis_heads = attend_local(vis_proj[0], vis_proj[1], vis_proj[2], vis_allowed)
    vis_heads, txt_out = lax.optimization_barrier((vis_heads, txt_out))
    txt_mine_full = lax.all_gather(core_half(txt_out)[0], "seq", axis=0, tiled=True)
    vis_attn = project_halves(heads_to_rows(vis_heads, seq_count), vis_mine_full, vis_other_full, core)
    residual_sum = patches.astype(jnp.float32) + vis_attn
    merged_in = (
        layer_norm(residual_sum, merge_gain)
        .astype(jnp.bfloat16)
        .reshape(token_count // 4, 4 * model_width)
    )
    feature_slices = lax.all_to_all(merged_in, "seq", split_axis=1, concat_axis=0, tiled=True)
    merge_partial = jnp.dot(feature_slices, merge_w, preferred_element_type=jnp.float32)
    merge_parts = lax.all_to_all(
        merge_partial.astype(jnp.bfloat16).reshape(seq_count, -1, model_width),
        "seq",
        split_axis=0,
        concat_axis=0,
        tiled=True,
    )
    visual = jnp.sum(merge_parts.astype(jnp.float32), axis=0).astype(jnp.bfloat16)
    dest_rows = dest_group[:, 0]
    merged_rows = dest_rows.shape[0]
    capacity = max(2, 2 * merged_rows // groups)
    onehot = (dest_rows[:, None] == jnp.arange(groups, dtype=jnp.int32)[None, :]).astype(jnp.int32)
    slot_rank = jnp.sum((jnp.cumsum(onehot, axis=0) - 1) * onehot, axis=1)
    selector = (
        (dest_rows[None, None, :] == jnp.arange(groups, dtype=jnp.int32)[:, None, None])
        & (slot_rank[None, None, :] == jnp.arange(capacity, dtype=jnp.int32)[None, :, None])
    ).astype(jnp.bfloat16)
    outgoing = jnp.einsum(
        "gct,td->gcd", selector, visual, preferred_element_type=jnp.float32
    ).astype(jnp.bfloat16)
    arrived_flags = jnp.sum(selector.astype(jnp.float32), axis=2).astype(jnp.bfloat16)
    flag_row = jnp.pad(arrived_flags, ((0, 0), (0, model_width - capacity)))[:, None, :]
    payload = lax.all_to_all(
        jnp.concatenate([outgoing, flag_row], axis=1), "grp", split_axis=0, concat_axis=0, tiled=True
    )
    incoming = payload[:, :capacity, :]
    arrived = payload[:, capacity, :capacity]
    prompt_rows = text_emb.shape[0]
    slot_targets = slot_rows[0, 0, : groups * capacity]
    placement_map = (
        slot_targets[None, :] == jnp.arange(prompt_rows, dtype=jnp.int32)[:, None]
    ).astype(jnp.bfloat16)
    placement_map = placement_map * arrived.reshape(1, groups * capacity)
    replaced = jnp.sum(placement_map.astype(jnp.float32), axis=1, keepdims=True)
    placed = jnp.dot(
        placement_map,
        incoming.reshape(groups * capacity, model_width),
        preferred_element_type=jnp.float32,
    )
    hidden = (text_emb.astype(jnp.float32) * (1.0 - replaced) + placed).astype(jnp.bfloat16)
    txt_normed = rms_norm(hidden, txt_gain).astype(jnp.bfloat16)
    txt_normed, txt_mine_full = lax.optimization_barrier((txt_normed, txt_mine_full))
    txt_other_full = swap_cores(txt_mine_full)
    txt_proj = projector(txt_qkv, lax.all_gather(txt_normed, "seq", axis=0, tiled=True))
    length = prompt_len[0]
    key_positions = jnp.arange(prompt_rows * seq_count, dtype=jnp.int32)

    def txt_allowed(row_indices):
        return (key_positions[None, :] <= row_indices[:, None]) & (key_positions[None, :] < length)

    txt_heads = attend_causal(txt_proj[0], txt_proj[1], txt_proj[2], txt_allowed)
    txt_attn = project_halves(heads_to_rows(txt_heads, seq_count), txt_mine_full, txt_other_full, core)
    return hidden.astype(jnp.float32) + txt_attn


def solution(mesh):
    in_specs = (
        P(("grp", "seq"), None),
        P(),
        P(None, None, "seq"),
        P("seq", None),
        P(),
        P("seq", None),
        P("grp", None),
        P(("grp", "seq"), None),
        P("grp", "seq", None),
        P("grp"),
        P(("grp", "seq"), None),
        P(),
        P(None, None, "seq"),
        P("seq", None),
    )
    out_specs = P(("grp", "seq"), None)
    return jax.shard_map(
        per_device, mesh=mesh, in_specs=in_specs, out_specs=out_specs, check_vma=False
    )
```

```python
import jax
import jax.numpy as jnp
from jax import lax
from jax.sharding import PartitionSpec as P

HEAD_DIM = 104


def layer_norm(row_block, scale_gain):
    values_f = row_block.astype(jnp.float32)
    row_mean = jnp.mean(values_f, axis=-1, keepdims=True)
    centred = values_f - row_mean
    variance = jnp.mean(centred * centred, axis=-1, keepdims=True)
    return centred * lax.rsqrt(variance + 1e-06) * scale_gain


def rms_norm(row_block, scale_gain):
    values_f = row_block.astype(jnp.float32)
    return (
        values_f
        * lax.rsqrt(jnp.mean(values_f * values_f, axis=-1, keepdims=True) + 1e-06)
        * scale_gain
    )


def projector(weights, shard_piece):
    return jnp.einsum(
        "rd,kde->kre", shard_piece, weights, preferred_element_type=jnp.float32
    ).astype(jnp.bfloat16)


def attend_local(queries, key_rows, value_rows, allowed_fn):
    length = queries.shape[0]
    head_width = queries.shape[1]
    head_count = head_width // HEAD_DIM
    block_rows = min(512, length)
    block_count = length // block_rows
    query_blocks = queries.reshape(block_count, block_rows, head_count, HEAD_DIM)
    key_heads = key_rows.reshape(length, head_count, HEAD_DIM)
    value_heads = value_rows.reshape(length, head_count, HEAD_DIM)

    def one_block(block_item):
        query_part, first_row = block_item
        scores = jnp.einsum(
            "qhe,khe->hqk", query_part, key_heads, preferred_element_type=jnp.float32
        ) * HEAD_DIM ** (-0.5)
        allowed = allowed_fn(first_row + jnp.arange(block_rows, dtype=jnp.int32))
        scores = jnp.where(allowed[None], scores, -1e30)
        row_max = jnp.max(scores, axis=-1, keepdims=True)
        expo = jnp.exp(scores - row_max)
        probabilities = (expo / jnp.sum(expo, axis=-1, keepdims=True)).astype(jnp.bfloat16)
        return jnp.einsum(
            "hqk,khe->qhe", probabilities, value_heads, preferred_element_type=jnp.float32
        ).astype(jnp.bfloat16)

    starts = jnp.arange(block_count, dtype=jnp.int32) * block_rows
    joined = lax.map(one_block, (query_blocks, starts))
    return joined.reshape(length, head_width)


def heads_to_rows(heads, seq_count):
    length, width = heads.shape
    rows = length // seq_count
    blocks = heads.reshape(seq_count, rows, width)
    swapped = lax.all_to_all(blocks, "seq", split_axis=0, concat_axis=0, tiled=True)
    return swapped.transpose(1, 0, 2).reshape(rows, seq_count * width)


def attend_causal(queries, key_rows, value_rows, allowed_fn):
    length = queries.shape[0]
    head_width = queries.shape[1]
    head_count = head_width // HEAD_DIM
    block_rows = min(512, length)
    block_count = length // block_rows
    key_heads = key_rows.reshape(length, head_count, HEAD_DIM)
    value_heads = value_rows.reshape(length, head_count, HEAD_DIM)
    outputs = []
    for block in range(block_count):
        first_row = block * block_rows
        key_end = first_row + block_rows
        query_part = queries[first_row:key_end].reshape(block_rows, head_count, HEAD_DIM)
        scores = jnp.einsum(
            "qhe,khe->hqk", query_part, key_heads[:key_end], preferred_element_type=jnp.float32
        ) * HEAD_DIM ** (-0.5)
        allowed = allowed_fn(first_row + jnp.arange(block_rows, dtype=jnp.int32))[:, :key_end]
        scores = jnp.where(allowed[None], scores, -1e30)
        row_max = jnp.max(scores, axis=-1, keepdims=True)
        expo = jnp.exp(scores - row_max)
        probabilities = (expo / jnp.sum(expo, axis=-1, keepdims=True)).astype(jnp.bfloat16)
        outputs.append(
            jnp.einsum(
                "hqk,khe->qhe", probabilities, value_heads[:key_end], preferred_element_type=jnp.float32
            ).astype(jnp.bfloat16)
        )
    return jnp.concatenate(outputs, axis=0).reshape(length, head_width)


def gather_row_half(w_local):
    half = w_local.shape[0] // 2
    groups = lax.axis_size("grp")
    core = lax.axis_index("grp") % 2
    mine = lax.dynamic_slice_in_dim(w_local, core * half, half, axis=0)
    mine_full = lax.all_gather(mine, "seq", axis=0, tiled=False)
    return mine_full, core


def swap_cores(mine_full):
    groups = lax.axis_size("grp")
    return lax.ppermute(mine_full, "grp", [(g, g ^ 1) for g in range(groups)])


def project_row_halves(rows, mine_full, other_full, core):
    count, half, width = mine_full.shape
    split = rows.reshape(rows.shape[0], count, 2, half)
    first, second = split[:, :, 0, :], split[:, :, 1, :]
    rows_mine = jnp.where(core == 0, first, second)
    rows_other = jnp.where(core == 0, second, first)
    return jnp.einsum(
        "rnh,nhd->rd", rows_mine, mine_full, preferred_element_type=jnp.float32
    ) + jnp.einsum("rnh,nhd->rd", rows_other, other_full, preferred_element_type=jnp.float32)


def per_device(
    patches,
    vis_gain,
    vis_qkv,
    vis_out,
    merge_gain,
    merge_w,
    image_blocks,
    dest_group,
    slot_rows,
    prompt_len,
    text_emb,
    txt_gain,
    txt_qkv,
    txt_out,
):
    seq_count = lax.axis_size("seq")
    groups = lax.axis_size("grp")
    token_count = patches.shape[0]
    model_width = patches.shape[1]
    group_patches = token_count * seq_count
    vis_normed = layer_norm(patches, vis_gain).astype(jnp.bfloat16)
    vis_gathered = lax.all_gather(vis_normed, "seq", axis=0, tiled=True)
    vis_gathered, vis_out = lax.optimization_barrier((vis_gathered, vis_out))
    vis_mine_full, core = gather_row_half(vis_out)
    vis_proj = projector(vis_qkv, vis_gathered)
    bounds = jnp.cumsum(image_blocks[0])[:-1]

    def segment(indices):
        return jnp.sum(((indices // 4)[:, None] >= bounds[None, :]).astype(jnp.int32), axis=1)

    key_segments = segment(jnp.arange(group_patches, dtype=jnp.int32))

    def vis_allowed(row_indices):
        return segment(row_indices)[:, None] == key_segments[None, :]

    vis_heads = attend_local(vis_proj[0], vis_proj[1], vis_proj[2], vis_allowed)
    vis_heads, txt_out = lax.optimization_barrier((vis_heads, txt_out))
    txt_mine_full = gather_row_half(txt_out)[0]
    vis_heads, vis_mine_full = lax.optimization_barrier((vis_heads, vis_mine_full))
    vis_other_full = swap_cores(vis_mine_full)
    vis_attn = project_row_halves(
        heads_to_rows(vis_heads, seq_count), vis_mine_full, vis_other_full, core
    )
    residual_sum = patches.astype(jnp.float32) + vis_attn
    merged_in = (
        layer_norm(residual_sum, merge_gain)
        .astype(jnp.bfloat16)
        .reshape(token_count // 4, 4 * model_width)
    )
    feature_slices = lax.all_to_all(merged_in, "seq", split_axis=1, concat_axis=0, tiled=True)
    merge_partial = jnp.dot(feature_slices, merge_w, preferred_element_type=jnp.float32)
    merge_parts = lax.all_to_all(
        merge_partial.astype(jnp.bfloat16).reshape(seq_count, -1, model_width),
        "seq",
        split_axis=0,
        concat_axis=0,
        tiled=True,
    )
    visual = jnp.sum(merge_parts.astype(jnp.float32), axis=0).astype(jnp.bfloat16)
    dest_rows = dest_group[:, 0]
    merged_rows = dest_rows.shape[0]
    capacity = max(2, 2 * merged_rows // groups)
    onehot = (dest_rows[:, None] == jnp.arange(groups, dtype=jnp.int32)[None, :]).astype(jnp.int32)
    slot_rank = jnp.sum((jnp.cumsum(onehot, axis=0) - 1) * onehot, axis=1)
    selector = (
        (dest_rows[None, None, :] == jnp.arange(groups, dtype=jnp.int32)[:, None, None])
        & (slot_rank[None, None, :] == jnp.arange(capacity, dtype=jnp.int32)[None, :, None])
    ).astype(jnp.bfloat16)
    outgoing = jnp.einsum(
        "gct,td->gcd", selector, visual, preferred_element_type=jnp.float32
    ).astype(jnp.bfloat16)
    arrived_flags = jnp.sum(selector.astype(jnp.float32), axis=2).astype(jnp.bfloat16)
    flag_row = jnp.pad(arrived_flags, ((0, 0), (0, model_width - capacity)))[:, None, :]
    payload = lax.all_to_all(
        jnp.concatenate([outgoing, flag_row], axis=1), "grp", split_axis=0, concat_axis=0, tiled=True
    )
    incoming = payload[:, :capacity, :]
    arrived = payload[:, capacity, :capacity]
    prompt_rows = text_emb.shape[0]
    slot_targets = slot_rows[0, 0, : groups * capacity]
    placement_map = (
        slot_targets[None, :] == jnp.arange(prompt_rows, dtype=jnp.int32)[:, None]
    ).astype(jnp.bfloat16)
    placement_map = placement_map * arrived.reshape(1, groups * capacity)
    replaced = jnp.sum(placement_map.astype(jnp.float32), axis=1, keepdims=True)
    placed = jnp.dot(
        placement_map,
        incoming.reshape(groups * capacity, model_width),
        preferred_element_type=jnp.float32,
    )
    hidden = (text_emb.astype(jnp.float32) * (1.0 - replaced) + placed).astype(jnp.bfloat16)
    txt_normed = rms_norm(hidden, txt_gain).astype(jnp.bfloat16)
    txt_normed, txt_mine_full = lax.optimization_barrier((txt_normed, txt_mine_full))
    txt_other_full = swap_cores(txt_mine_full)
    txt_proj = projector(txt_qkv, lax.all_gather(txt_normed, "seq", axis=0, tiled=True))
    length = prompt_len[0]
    key_positions = jnp.arange(prompt_rows * seq_count, dtype=jnp.int32)

    def txt_allowed(row_indices):
        return (key_positions[None, :] <= row_indices[:, None]) & (key_positions[None, :] < length)

    txt_heads = attend_causal(txt_proj[0], txt_proj[1], txt_proj[2], txt_allowed)
    txt_attn = project_row_halves(
        heads_to_rows(txt_heads, seq_count), txt_mine_full, txt_other_full, core
    )
    return hidden.astype(jnp.float32) + txt_attn


def solution(mesh):
    in_specs = (
        P(("grp", "seq"), None),
        P(),
        P(None, None, "seq"),
        P("seq", None),
        P(),
        P("seq", None),
        P("grp", None),
        P(("grp", "seq"), None),
        P("grp", "seq", None),
        P("grp"),
        P(("grp", "seq"), None),
        P(),
        P(None, None, "seq"),
        P("seq", None),
    )
    out_specs = P(("grp", "seq"), None)
    return jax.shard_map(
        per_device, mesh=mesh, in_specs=in_specs, out_specs=out_specs, check_vma=False
    )
```

```python
import jax
import jax.numpy as jnp
from jax import lax
from jax.sharding import PartitionSpec as P

HEAD_DIM = 104


def layer_norm(row_block, scale_gain):
    values_f = row_block.astype(jnp.float32)
    row_mean = jnp.mean(values_f, axis=-1, keepdims=True)
    centred = values_f - row_mean
    variance = jnp.mean(centred * centred, axis=-1, keepdims=True)
    return centred * lax.rsqrt(variance + 1e-06) * scale_gain


def rms_norm(row_block, scale_gain):
    values_f = row_block.astype(jnp.float32)
    return (
        values_f
        * lax.rsqrt(jnp.mean(values_f * values_f, axis=-1, keepdims=True) + 1e-06)
        * scale_gain
    )


def projector(weights, shard_piece):
    return jnp.einsum(
        "rd,kde->kre", shard_piece, weights, preferred_element_type=jnp.float32
    ).astype(jnp.bfloat16)


def attend_local(queries, key_rows, value_rows, allowed_fn):
    length = queries.shape[0]
    head_width = queries.shape[1]
    head_count = head_width // HEAD_DIM
    block_rows = min(512, length)
    block_count = length // block_rows
    query_blocks = queries.reshape(block_count, block_rows, head_count, HEAD_DIM)
    key_heads = key_rows.reshape(length, head_count, HEAD_DIM)
    value_heads = value_rows.reshape(length, head_count, HEAD_DIM)

    def one_block(block_item):
        query_part, first_row = block_item
        scores = jnp.einsum(
            "qhe,khe->hqk", query_part, key_heads, preferred_element_type=jnp.float32
        ) * HEAD_DIM ** (-0.5)
        allowed = allowed_fn(first_row + jnp.arange(block_rows, dtype=jnp.int32))
        scores = jnp.where(allowed[None], scores, -1e30)
        row_max = jnp.max(scores, axis=-1, keepdims=True)
        expo = jnp.exp(scores - row_max)
        probabilities = (expo / jnp.sum(expo, axis=-1, keepdims=True)).astype(jnp.bfloat16)
        return jnp.einsum(
            "hqk,khe->qhe", probabilities, value_heads, preferred_element_type=jnp.float32
        ).astype(jnp.bfloat16)

    starts = jnp.arange(block_count, dtype=jnp.int32) * block_rows
    joined = lax.map(one_block, (query_blocks, starts))
    return joined.reshape(length, head_width)


def heads_to_rows(heads, seq_count):
    length, width = heads.shape
    rows = length // seq_count
    blocks = heads.reshape(seq_count, rows, width)
    swapped = lax.all_to_all(blocks, "seq", split_axis=0, concat_axis=0, tiled=True)
    return swapped.transpose(1, 0, 2).reshape(rows, seq_count * width)


def attend_causal(queries, key_rows, value_rows, allowed_fn):
    length = queries.shape[0]
    head_width = queries.shape[1]
    head_count = head_width // HEAD_DIM
    block_rows = min(512, length)
    block_count = length // block_rows
    key_heads = key_rows.reshape(length, head_count, HEAD_DIM)
    value_heads = value_rows.reshape(length, head_count, HEAD_DIM)
    outputs = []
    for block in range(block_count):
        first_row = block * block_rows
        key_end = first_row + block_rows
        query_part = queries[first_row:key_end].reshape(block_rows, head_count, HEAD_DIM)
        scores = jnp.einsum(
            "qhe,khe->hqk", query_part, key_heads[:key_end], preferred_element_type=jnp.float32
        ) * HEAD_DIM ** (-0.5)
        allowed = allowed_fn(first_row + jnp.arange(block_rows, dtype=jnp.int32))[:, :key_end]
        scores = jnp.where(allowed[None], scores, -1e30)
        row_max = jnp.max(scores, axis=-1, keepdims=True)
        expo = jnp.exp(scores - row_max)
        probabilities = (expo / jnp.sum(expo, axis=-1, keepdims=True)).astype(jnp.bfloat16)
        outputs.append(
            jnp.einsum(
                "hqk,khe->qhe", probabilities, value_heads[:key_end], preferred_element_type=jnp.float32
            ).astype(jnp.bfloat16)
        )
    return jnp.concatenate(outputs, axis=0).reshape(length, head_width)


def split_gather(rows_local, seq_count):
    first = rows_local.shape[0] * 5 // 8 // 16 * 16
    gathered = lax.all_gather(rows_local[:first], "seq", axis=0, tiled=False)
    rest = rows_local[first:]
    copies = jnp.broadcast_to(rest[None], (seq_count,) + rest.shape)
    exchanged = lax.all_to_all(copies, "seq", split_axis=0, concat_axis=0, tiled=True)
    return gathered, exchanged


def split_project(weights, pieces):
    outs = [
        jnp.einsum("srd,kde->ksre", piece, weights, preferred_element_type=jnp.float32).astype(
            jnp.bfloat16
        )
        for piece in pieces
    ]
    joined = jnp.concatenate(outs, axis=2)
    return joined.reshape(joined.shape[0], -1, joined.shape[-1])


def per_device(
    patches,
    vis_gain,
    vis_qkv,
    vis_out,
    merge_gain,
    merge_w,
    image_blocks,
    dest_group,
    slot_rows,
    prompt_len,
    text_emb,
    txt_gain,
    txt_qkv,
    txt_out,
):
    seq_count = lax.axis_size("seq")
    groups = lax.axis_size("grp")
    token_count = patches.shape[0]
    model_width = patches.shape[1]
    group_patches = token_count * seq_count
    vis_out_full = lax.all_gather(vis_out, "seq", axis=0, tiled=True)
    vis_normed = layer_norm(patches, vis_gain).astype(jnp.bfloat16)
    vis_proj = split_project(vis_qkv, split_gather(vis_normed, seq_count))
    bounds = jnp.cumsum(image_blocks[0])[:-1]

    def segment(indices):
        return jnp.sum(((indices // 4)[:, None] >= bounds[None, :]).astype(jnp.int32), axis=1)

    key_segments = segment(jnp.arange(group_patches, dtype=jnp.int32))

    def vis_allowed(row_indices):
        return segment(row_indices)[:, None] == key_segments[None, :]

    vis_heads = attend_local(vis_proj[0], vis_proj[1], vis_proj[2], vis_allowed)
    vis_heads, txt_out = lax.optimization_barrier((vis_heads, txt_out))
    txt_out_full = lax.all_gather(txt_out, "seq", axis=0, tiled=True)
    vis_attn = jnp.dot(
        heads_to_rows(vis_heads, seq_count), vis_out_full, preferred_element_type=jnp.float32
    )
    residual_sum = patches.astype(jnp.float32) + vis_attn
    merged_in = (
        layer_norm(residual_sum, merge_gain)
        .astype(jnp.bfloat16)
        .reshape(token_count // 4, 4 * model_width)
    )
    feature_slices = lax.all_to_all(merged_in, "seq", split_axis=1, concat_axis=0, tiled=True)
    merge_partial = jnp.dot(feature_slices, merge_w, preferred_element_type=jnp.float32)
    merge_parts = lax.all_to_all(
        merge_partial.astype(jnp.bfloat16).reshape(seq_count, -1, model_width),
        "seq",
        split_axis=0,
        concat_axis=0,
        tiled=True,
    )
    visual = jnp.sum(merge_parts.astype(jnp.float32), axis=0).astype(jnp.bfloat16)
    dest_rows = dest_group[:, 0]
    merged_rows = dest_rows.shape[0]
    capacity = max(2, 2 * merged_rows // groups)
    onehot = (dest_rows[:, None] == jnp.arange(groups, dtype=jnp.int32)[None, :]).astype(jnp.int32)
    slot_rank = jnp.sum((jnp.cumsum(onehot, axis=0) - 1) * onehot, axis=1)
    selector = (
        (dest_rows[None, None, :] == jnp.arange(groups, dtype=jnp.int32)[:, None, None])
        & (slot_rank[None, None, :] == jnp.arange(capacity, dtype=jnp.int32)[None, :, None])
    ).astype(jnp.bfloat16)
    outgoing = jnp.einsum(
        "gct,td->gcd", selector, visual, preferred_element_type=jnp.float32
    ).astype(jnp.bfloat16)
    arrived_flags = jnp.sum(selector.astype(jnp.float32), axis=2).astype(jnp.bfloat16)
    flag_row = jnp.pad(arrived_flags, ((0, 0), (0, model_width - capacity)))[:, None, :]
    payload = lax.all_to_all(
        jnp.concatenate([outgoing, flag_row], axis=1), "grp", split_axis=0, concat_axis=0, tiled=True
    )
    incoming = payload[:, :capacity, :]
    arrived = payload[:, capacity, :capacity]
    prompt_rows = text_emb.shape[0]
    slot_targets = slot_rows[0, 0, : groups * capacity]
    placement_map = (
        slot_targets[None, :] == jnp.arange(prompt_rows, dtype=jnp.int32)[:, None]
    ).astype(jnp.bfloat16)
    placement_map = placement_map * arrived.reshape(1, groups * capacity)
    replaced = jnp.sum(placement_map.astype(jnp.float32), axis=1, keepdims=True)
    placed = jnp.dot(
        placement_map,
        incoming.reshape(groups * capacity, model_width),
        preferred_element_type=jnp.float32,
    )
    hidden = (text_emb.astype(jnp.float32) * (1.0 - replaced) + placed).astype(jnp.bfloat16)
    txt_normed = rms_norm(hidden, txt_gain).astype(jnp.bfloat16)
    txt_normed, txt_out_full = lax.optimization_barrier((txt_normed, txt_out_full))
    txt_proj = split_project(txt_qkv, split_gather(txt_normed, seq_count))
    length = prompt_len[0]
    key_positions = jnp.arange(prompt_rows * seq_count, dtype=jnp.int32)

    def txt_allowed(row_indices):
        return (key_positions[None, :] <= row_indices[:, None]) & (key_positions[None, :] < length)

    txt_heads = attend_causal(txt_proj[0], txt_proj[1], txt_proj[2], txt_allowed)
    txt_attn = jnp.dot(
        heads_to_rows(txt_heads, seq_count), txt_out_full, preferred_element_type=jnp.float32
    )
    return hidden.astype(jnp.float32) + txt_attn


def solution(mesh):
    in_specs = (
        P(("grp", "seq"), None),
        P(),
        P(None, None, "seq"),
        P("seq", None),
        P(),
        P("seq", None),
        P("grp", None),
        P(("grp", "seq"), None),
        P("grp", "seq", None),
        P("grp"),
        P(("grp", "seq"), None),
        P(),
        P(None, None, "seq"),
        P("seq", None),
    )
    out_specs = P(("grp", "seq"), None)
    return jax.shard_map(
        per_device, mesh=mesh, in_specs=in_specs, out_specs=out_specs, check_vma=False
    )
```

```python
import jax
import jax.numpy as jnp
from jax import lax
from jax.sharding import PartitionSpec as P

HEAD_DIM = 104


def layer_norm(row_block, scale_gain):
    values_f = row_block.astype(jnp.float32)
    row_mean = jnp.mean(values_f, axis=-1, keepdims=True)
    centred = values_f - row_mean
    variance = jnp.mean(centred * centred, axis=-1, keepdims=True)
    return centred * lax.rsqrt(variance + 1e-06) * scale_gain


def rms_norm(row_block, scale_gain):
    values_f = row_block.astype(jnp.float32)
    return (
        values_f
        * lax.rsqrt(jnp.mean(values_f * values_f, axis=-1, keepdims=True) + 1e-06)
        * scale_gain
    )


def projector(weights, shard_piece):
    count, width, head_width = weights.shape
    packed = weights.transpose(1, 0, 2).reshape(width, count * head_width)
    joined = jnp.dot(shard_piece, packed, preferred_element_type=jnp.float32).astype(jnp.bfloat16)
    return joined.reshape(shard_piece.shape[0], count, head_width).transpose(1, 0, 2)


def attend_local(queries, key_rows, value_rows, allowed_fn):
    length = queries.shape[0]
    head_width = queries.shape[1]
    head_count = head_width // HEAD_DIM
    block_rows = min(512, length)
    block_count = length // block_rows
    query_blocks = queries.reshape(block_count, block_rows, head_count, HEAD_DIM)
    key_heads = key_rows.reshape(length, head_count, HEAD_DIM)
    value_heads = value_rows.reshape(length, head_count, HEAD_DIM)

    def one_block(block_item):
        query_part, first_row = block_item
        scores = jnp.einsum(
            "qhe,khe->hqk", query_part, key_heads, preferred_element_type=jnp.float32
        ) * HEAD_DIM ** (-0.5)
        allowed = allowed_fn(first_row + jnp.arange(block_rows, dtype=jnp.int32))
        scores = jnp.where(allowed[None], scores, -1e30)
        row_max = jnp.max(scores, axis=-1, keepdims=True)
        expo = jnp.exp(scores - row_max)
        probabilities = (expo / jnp.sum(expo, axis=-1, keepdims=True)).astype(jnp.bfloat16)
        return jnp.einsum(
            "hqk,khe->qhe", probabilities, value_heads, preferred_element_type=jnp.float32
        ).astype(jnp.bfloat16)

    starts = jnp.arange(block_count, dtype=jnp.int32) * block_rows
    joined = lax.map(one_block, (query_blocks, starts))
    return joined.reshape(length, head_width)


def heads_to_rows(heads, seq_count):
    length, width = heads.shape
    rows = length // seq_count
    blocks = heads.reshape(seq_count, rows, width)
    swapped = lax.all_to_all(blocks, "seq", split_axis=0, concat_axis=0, tiled=True)
    return swapped.transpose(1, 0, 2).reshape(rows, seq_count * width)


def attend_causal(queries, key_rows, value_rows, allowed_fn):
    length = queries.shape[0]
    head_width = queries.shape[1]
    head_count = head_width // HEAD_DIM
    block_rows = min(512, length)
    block_count = length // block_rows
    key_heads = key_rows.reshape(length, head_count, HEAD_DIM)
    value_heads = value_rows.reshape(length, head_count, HEAD_DIM)
    outputs = []
    for block in range(block_count):
        first_row = block * block_rows
        key_end = first_row + block_rows
        query_part = queries[first_row:key_end].reshape(block_rows, head_count, HEAD_DIM)
        scores = jnp.einsum(
            "qhe,khe->hqk", query_part, key_heads[:key_end], preferred_element_type=jnp.float32
        ) * HEAD_DIM ** (-0.5)
        allowed = allowed_fn(first_row + jnp.arange(block_rows, dtype=jnp.int32))[:, :key_end]
        scores = jnp.where(allowed[None], scores, -1e30)
        row_max = jnp.max(scores, axis=-1, keepdims=True)
        expo = jnp.exp(scores - row_max)
        probabilities = (expo / jnp.sum(expo, axis=-1, keepdims=True)).astype(jnp.bfloat16)
        outputs.append(
            jnp.einsum(
                "hqk,khe->qhe", probabilities, value_heads[:key_end], preferred_element_type=jnp.float32
            ).astype(jnp.bfloat16)
        )
    return jnp.concatenate(outputs, axis=0).reshape(length, head_width)


def per_device(
    patches,
    vis_gain,
    vis_qkv,
    vis_out,
    merge_gain,
    merge_w,
    image_blocks,
    dest_group,
    slot_rows,
    prompt_len,
    text_emb,
    txt_gain,
    txt_qkv,
    txt_out,
):
    seq_count = lax.axis_size("seq")
    groups = lax.axis_size("grp")
    token_count = patches.shape[0]
    model_width = patches.shape[1]
    group_patches = token_count * seq_count
    vis_out_full = lax.all_gather(vis_out, "seq", axis=0, tiled=True)
    vis_normed = layer_norm(patches, vis_gain).astype(jnp.bfloat16)
    vis_proj = projector(vis_qkv, lax.all_gather(vis_normed, "seq", axis=0, tiled=True))
    bounds = jnp.cumsum(image_blocks[0])[:-1]

    def segment(indices):
        return jnp.sum(((indices // 4)[:, None] >= bounds[None, :]).astype(jnp.int32), axis=1)

    key_segments = segment(jnp.arange(group_patches, dtype=jnp.int32))

    def vis_allowed(row_indices):
        return segment(row_indices)[:, None] == key_segments[None, :]

    vis_heads = attend_local(vis_proj[0], vis_proj[1], vis_proj[2], vis_allowed)
    vis_heads, txt_out = lax.optimization_barrier((vis_heads, txt_out))
    txt_out_full = lax.all_gather(txt_out, "seq", axis=0, tiled=True)
    vis_attn = jnp.dot(
        heads_to_rows(vis_heads, seq_count), vis_out_full, preferred_element_type=jnp.float32
    )
    residual_sum = patches.astype(jnp.float32) + vis_attn
    merged_in = (
        layer_norm(residual_sum, merge_gain)
        .astype(jnp.bfloat16)
        .reshape(token_count // 4, 4 * model_width)
    )
    feature_slices = lax.all_to_all(merged_in, "seq", split_axis=1, concat_axis=0, tiled=True)
    merge_partial = jnp.dot(feature_slices, merge_w, preferred_element_type=jnp.float32)
    merge_parts = lax.all_to_all(
        merge_partial.astype(jnp.bfloat16).reshape(seq_count, -1, model_width),
        "seq",
        split_axis=0,
        concat_axis=0,
        tiled=True,
    )
    visual = jnp.sum(merge_parts.astype(jnp.float32), axis=0).astype(jnp.bfloat16)
    dest_rows = dest_group[:, 0]
    merged_rows = dest_rows.shape[0]
    capacity = max(2, 2 * merged_rows // groups)
    onehot = (dest_rows[:, None] == jnp.arange(groups, dtype=jnp.int32)[None, :]).astype(jnp.int32)
    slot_rank = jnp.sum((jnp.cumsum(onehot, axis=0) - 1) * onehot, axis=1)
    selector = (
        (dest_rows[None, None, :] == jnp.arange(groups, dtype=jnp.int32)[:, None, None])
        & (slot_rank[None, None, :] == jnp.arange(capacity, dtype=jnp.int32)[None, :, None])
    ).astype(jnp.bfloat16)
    outgoing = jnp.einsum(
        "gct,td->gcd", selector, visual, preferred_element_type=jnp.float32
    ).astype(jnp.bfloat16)
    arrived_flags = jnp.sum(selector.astype(jnp.float32), axis=2).astype(jnp.bfloat16)
    flag_row = jnp.pad(arrived_flags, ((0, 0), (0, model_width - capacity)))[:, None, :]
    payload = lax.all_to_all(
        jnp.concatenate([outgoing, flag_row], axis=1), "grp", split_axis=0, concat_axis=0, tiled=True
    )
    incoming = payload[:, :capacity, :]
    arrived = payload[:, capacity, :capacity]
    prompt_rows = text_emb.shape[0]
    slot_targets = slot_rows[0, 0, : groups * capacity]
    placement_map = (
        slot_targets[None, :] == jnp.arange(prompt_rows, dtype=jnp.int32)[:, None]
    ).astype(jnp.bfloat16)
    placement_map = placement_map * arrived.reshape(1, groups * capacity)
    replaced = jnp.sum(placement_map.astype(jnp.float32), axis=1, keepdims=True)
    placed = jnp.dot(
        placement_map,
        incoming.reshape(groups * capacity, model_width),
        preferred_element_type=jnp.float32,
    )
    hidden = (text_emb.astype(jnp.float32) * (1.0 - replaced) + placed).astype(jnp.bfloat16)
    txt_normed = rms_norm(hidden, txt_gain).astype(jnp.bfloat16)
    txt_normed, txt_out_full = lax.optimization_barrier((txt_normed, txt_out_full))
    txt_proj = projector(txt_qkv, lax.all_gather(txt_normed, "seq", axis=0, tiled=True))
    length = prompt_len[0]
    key_positions = jnp.arange(prompt_rows * seq_count, dtype=jnp.int32)

    def txt_allowed(row_indices):
        return (key_positions[None, :] <= row_indices[:, None]) & (key_positions[None, :] < length)

    txt_heads = attend_causal(txt_proj[0], txt_proj[1], txt_proj[2], txt_allowed)
    txt_attn = jnp.dot(
        heads_to_rows(txt_heads, seq_count), txt_out_full, preferred_element_type=jnp.float32
    )
    return hidden.astype(jnp.float32) + txt_attn


def solution(mesh):
    in_specs = (
        P(("grp", "seq"), None),
        P(),
        P(None, None, "seq"),
        P("seq", None),
        P(),
        P("seq", None),
        P("grp", None),
        P(("grp", "seq"), None),
        P("grp", "seq", None),
        P("grp"),
        P(("grp", "seq"), None),
        P(),
        P(None, None, "seq"),
        P("seq", None),
    )
    out_specs = P(("grp", "seq"), None)
    return jax.shard_map(
        per_device, mesh=mesh, in_specs=in_specs, out_specs=out_specs, check_vma=False
    )
```

```python
import jax
import jax.numpy as jnp
from jax.experimental import pallas as pl
from jax.experimental.pallas import tpu as pltpu
from jax import lax
from jax.sharding import PartitionSpec as P

HEAD_DIM = 104


def layer_norm(row_block, scale_gain):
    values_f = row_block.astype(jnp.float32)
    row_mean = jnp.mean(values_f, axis=-1, keepdims=True)
    centred = values_f - row_mean
    variance = jnp.mean(centred * centred, axis=-1, keepdims=True)
    return centred * lax.rsqrt(variance + 1e-06) * scale_gain


def layer_norm_kernel(x_ref, g_ref, o_ref):
    values_f = x_ref[...].astype(jnp.float32)
    row_mean = jnp.mean(values_f, axis=-1, keepdims=True)
    centred = values_f - row_mean
    variance = jnp.mean(centred * centred, axis=-1, keepdims=True)
    o_ref[...] = (centred * lax.rsqrt(variance + 1e-06) * g_ref[...]).astype(o_ref.dtype)


def layer_norm_fused(row_block, scale_gain):
    rows, width = row_block.shape
    return pl.pallas_call(
        layer_norm_kernel,
        out_shape=jax.ShapeDtypeStruct((rows, width), jnp.bfloat16),
        in_specs=[pl.BlockSpec(memory_space=pltpu.VMEM)] * 2,
        out_specs=pl.BlockSpec(memory_space=pltpu.VMEM),
        cost_estimate=pl.CostEstimate(
            flops=8 * rows * width, transcendentals=rows, bytes_accessed=4 * rows * width + 4 * width
        ),
    )(row_block, scale_gain.reshape(1, width))


def rms_norm(row_block, scale_gain):
    values_f = row_block.astype(jnp.float32)
    return (
        values_f
        * lax.rsqrt(jnp.mean(values_f * values_f, axis=-1, keepdims=True) + 1e-06)
        * scale_gain
    )


def projector(weights, shard_piece):
    count, width, head_width = weights.shape
    packed = weights.transpose(1, 0, 2).reshape(width, count * head_width)
    joined = jnp.dot(shard_piece, packed, preferred_element_type=jnp.float32).astype(jnp.bfloat16)
    return joined.reshape(shard_piece.shape[0], count, head_width).transpose(1, 0, 2)


def attend_local(queries, key_rows, value_rows, allowed_fn):
    length = queries.shape[0]
    head_width = queries.shape[1]
    head_count = head_width // HEAD_DIM
    block_rows = min(512, length)
    block_count = length // block_rows
    query_blocks = queries.reshape(block_count, block_rows, head_count, HEAD_DIM)
    key_heads = key_rows.reshape(length, head_count, HEAD_DIM)
    value_heads = value_rows.reshape(length, head_count, HEAD_DIM)

    def one_block(block_item):
        query_part, first_row = block_item
        scores = jnp.einsum(
            "qhe,khe->hqk", query_part, key_heads, preferred_element_type=jnp.float32
        ) * HEAD_DIM ** (-0.5)
        allowed = allowed_fn(first_row + jnp.arange(block_rows, dtype=jnp.int32))
        scores = jnp.where(allowed[None], scores, -1e30)
        row_max = jnp.max(scores, axis=-1, keepdims=True)
        expo = jnp.exp(scores - row_max)
        probabilities = (expo / jnp.sum(expo, axis=-1, keepdims=True)).astype(jnp.bfloat16)
        return jnp.einsum(
            "hqk,khe->qhe", probabilities, value_heads, preferred_element_type=jnp.float32
        ).astype(jnp.bfloat16)

    starts = jnp.arange(block_count, dtype=jnp.int32) * block_rows
    joined = lax.map(one_block, (query_blocks, starts))
    return joined.reshape(length, head_width)


def heads_to_rows(heads, seq_count):
    length, width = heads.shape
    rows = length // seq_count
    blocks = heads.reshape(seq_count, rows, width)
    swapped = lax.all_to_all(blocks, "seq", split_axis=0, concat_axis=0, tiled=True)
    return swapped.transpose(1, 0, 2).reshape(rows, seq_count * width)


def attend_causal(queries, key_rows, value_rows, allowed_fn):
    length = queries.shape[0]
    head_width = queries.shape[1]
    head_count = head_width // HEAD_DIM
    block_rows = min(512, length)
    block_count = length // block_rows
    key_heads = key_rows.reshape(length, head_count, HEAD_DIM)
    value_heads = value_rows.reshape(length, head_count, HEAD_DIM)
    outputs = []
    for block in range(block_count):
        first_row = block * block_rows
        key_end = first_row + block_rows
        query_part = queries[first_row:key_end].reshape(block_rows, head_count, HEAD_DIM)
        scores = jnp.einsum(
            "qhe,khe->hqk", query_part, key_heads[:key_end], preferred_element_type=jnp.float32
        ) * HEAD_DIM ** (-0.5)
        allowed = allowed_fn(first_row + jnp.arange(block_rows, dtype=jnp.int32))[:, :key_end]
        scores = jnp.where(allowed[None], scores, -1e30)
        row_max = jnp.max(scores, axis=-1, keepdims=True)
        expo = jnp.exp(scores - row_max)
        probabilities = (expo / jnp.sum(expo, axis=-1, keepdims=True)).astype(jnp.bfloat16)
        outputs.append(
            jnp.einsum(
                "hqk,khe->qhe", probabilities, value_heads[:key_end], preferred_element_type=jnp.float32
            ).astype(jnp.bfloat16)
        )
    return jnp.concatenate(outputs, axis=0).reshape(length, head_width)


def per_device(
    patches,
    vis_gain,
    vis_qkv,
    vis_out,
    merge_gain,
    merge_w,
    image_blocks,
    dest_group,
    slot_rows,
    prompt_len,
    text_emb,
    txt_gain,
    txt_qkv,
    txt_out,
):
    seq_count = lax.axis_size("seq")
    groups = lax.axis_size("grp")
    token_count = patches.shape[0]
    model_width = patches.shape[1]
    group_patches = token_count * seq_count
    vis_out_full = lax.all_gather(vis_out, "seq", axis=0, tiled=True)
    vis_normed = layer_norm_fused(patches, vis_gain)
    vis_proj = projector(vis_qkv, lax.all_gather(vis_normed, "seq", axis=0, tiled=True))
    bounds = jnp.cumsum(image_blocks[0])[:-1]

    def segment(indices):
        return jnp.sum(((indices // 4)[:, None] >= bounds[None, :]).astype(jnp.int32), axis=1)

    key_segments = segment(jnp.arange(group_patches, dtype=jnp.int32))

    def vis_allowed(row_indices):
        return segment(row_indices)[:, None] == key_segments[None, :]

    vis_heads = attend_local(vis_proj[0], vis_proj[1], vis_proj[2], vis_allowed)
    vis_heads, txt_out = lax.optimization_barrier((vis_heads, txt_out))
    txt_out_full = lax.all_gather(txt_out, "seq", axis=0, tiled=True)
    vis_attn = jnp.dot(
        heads_to_rows(vis_heads, seq_count), vis_out_full, preferred_element_type=jnp.float32
    )
    residual_sum = patches.astype(jnp.float32) + vis_attn
    merged_in = (
        layer_norm(residual_sum, merge_gain)
        .astype(jnp.bfloat16)
        .reshape(token_count // 4, 4 * model_width)
    )
    feature_slices = lax.all_to_all(merged_in, "seq", split_axis=1, concat_axis=0, tiled=True)
    merge_partial = jnp.dot(feature_slices, merge_w, preferred_element_type=jnp.float32)
    merge_parts = lax.all_to_all(
        merge_partial.astype(jnp.bfloat16).reshape(seq_count, -1, model_width),
        "seq",
        split_axis=0,
        concat_axis=0,
        tiled=True,
    )
    visual = jnp.sum(merge_parts.astype(jnp.float32), axis=0).astype(jnp.bfloat16)
    dest_rows = dest_group[:, 0]
    merged_rows = dest_rows.shape[0]
    capacity = max(2, 2 * merged_rows // groups)
    onehot = (dest_rows[:, None] == jnp.arange(groups, dtype=jnp.int32)[None, :]).astype(jnp.int32)
    slot_rank = jnp.sum((jnp.cumsum(onehot, axis=0) - 1) * onehot, axis=1)
    selector = (
        (dest_rows[None, None, :] == jnp.arange(groups, dtype=jnp.int32)[:, None, None])
        & (slot_rank[None, None, :] == jnp.arange(capacity, dtype=jnp.int32)[None, :, None])
    ).astype(jnp.bfloat16)
    outgoing = jnp.einsum(
        "gct,td->gcd", selector, visual, preferred_element_type=jnp.float32
    ).astype(jnp.bfloat16)
    arrived_flags = jnp.sum(selector.astype(jnp.float32), axis=2).astype(jnp.bfloat16)
    flag_row = jnp.pad(arrived_flags, ((0, 0), (0, model_width - capacity)))[:, None, :]
    payload = lax.all_to_all(
        jnp.concatenate([outgoing, flag_row], axis=1), "grp", split_axis=0, concat_axis=0, tiled=True
    )
    incoming = payload[:, :capacity, :]
    arrived = payload[:, capacity, :capacity]
    prompt_rows = text_emb.shape[0]
    slot_targets = slot_rows[0, 0, : groups * capacity]
    placement_map = (
        slot_targets[None, :] == jnp.arange(prompt_rows, dtype=jnp.int32)[:, None]
    ).astype(jnp.bfloat16)
    placement_map = placement_map * arrived.reshape(1, groups * capacity)
    replaced = jnp.sum(placement_map.astype(jnp.float32), axis=1, keepdims=True)
    placed = jnp.dot(
        placement_map,
        incoming.reshape(groups * capacity, model_width),
        preferred_element_type=jnp.float32,
    )
    hidden = (text_emb.astype(jnp.float32) * (1.0 - replaced) + placed).astype(jnp.bfloat16)
    txt_normed = rms_norm(hidden, txt_gain).astype(jnp.bfloat16)
    txt_normed, txt_out_full = lax.optimization_barrier((txt_normed, txt_out_full))
    txt_proj = projector(txt_qkv, lax.all_gather(txt_normed, "seq", axis=0, tiled=True))
    length = prompt_len[0]
    key_positions = jnp.arange(prompt_rows * seq_count, dtype=jnp.int32)

    def txt_allowed(row_indices):
        return (key_positions[None, :] <= row_indices[:, None]) & (key_positions[None, :] < length)

    txt_heads = attend_causal(txt_proj[0], txt_proj[1], txt_proj[2], txt_allowed)
    txt_attn = jnp.dot(
        heads_to_rows(txt_heads, seq_count), txt_out_full, preferred_element_type=jnp.float32
    )
    return hidden.astype(jnp.float32) + txt_attn


def solution(mesh):
    in_specs = (
        P(("grp", "seq"), None),
        P(),
        P(None, None, "seq"),
        P("seq", None),
        P(),
        P("seq", None),
        P("grp", None),
        P(("grp", "seq"), None),
        P("grp", "seq", None),
        P("grp"),
        P(("grp", "seq"), None),
        P(),
        P(None, None, "seq"),
        P("seq", None),
    )
    out_specs = P(("grp", "seq"), None)
    return jax.shard_map(
        per_device, mesh=mesh, in_specs=in_specs, out_specs=out_specs, check_vma=False
    )
```

```python
import jax
import jax.numpy as jnp
from jax.experimental import pallas as pl
from jax.experimental.pallas import tpu as pltpu
from jax import lax
from jax.sharding import PartitionSpec as P

HEAD_DIM = 104


def layer_norm(row_block, scale_gain):
    values_f = row_block.astype(jnp.float32)
    row_mean = jnp.mean(values_f, axis=-1, keepdims=True)
    centred = values_f - row_mean
    variance = jnp.mean(centred * centred, axis=-1, keepdims=True)
    return centred * lax.rsqrt(variance + 1e-06) * scale_gain


def layer_norm_kernel(x_ref, g_ref, o_ref):
    values_f = x_ref[...].astype(jnp.float32)
    row_mean = jnp.mean(values_f, axis=-1, keepdims=True)
    centred = values_f - row_mean
    variance = jnp.mean(centred * centred, axis=-1, keepdims=True)
    o_ref[...] = (centred * lax.rsqrt(variance + 1e-06) * g_ref[...][None, :]).astype(o_ref.dtype)


def layer_norm_fused(row_block, scale_gain):
    rows, width = row_block.shape
    return pl.pallas_call(
        layer_norm_kernel,
        out_shape=jax.ShapeDtypeStruct((rows, width), jnp.bfloat16),
        in_specs=[pl.BlockSpec(memory_space=pltpu.VMEM)] * 2,
        out_specs=pl.BlockSpec(memory_space=pltpu.VMEM),
        cost_estimate=pl.CostEstimate(
            flops=8 * rows * width, transcendentals=rows, bytes_accessed=4 * rows * width + 4 * width
        ),
    )(row_block, scale_gain)


def rms_norm(row_block, scale_gain):
    values_f = row_block.astype(jnp.float32)
    return (
        values_f
        * lax.rsqrt(jnp.mean(values_f * values_f, axis=-1, keepdims=True) + 1e-06)
        * scale_gain
    )


def projector(weights, shard_piece):
    count, width, head_width = weights.shape
    packed = weights.transpose(1, 0, 2).reshape(width, count * head_width)
    joined = jnp.dot(shard_piece, packed, preferred_element_type=jnp.float32).astype(jnp.bfloat16)
    return joined.reshape(shard_piece.shape[0], count, head_width).transpose(1, 0, 2)


def attend_local(queries, key_rows, value_rows, allowed_fn):
    length = queries.shape[0]
    head_width = queries.shape[1]
    head_count = head_width // HEAD_DIM
    block_rows = min(512, length)
    block_count = length // block_rows
    query_blocks = queries.reshape(block_count, block_rows, head_count, HEAD_DIM)
    key_heads = key_rows.reshape(length, head_count, HEAD_DIM)
    value_heads = value_rows.reshape(length, head_count, HEAD_DIM)

    def one_block(block_item):
        query_part, first_row = block_item
        scores = jnp.einsum(
            "qhe,khe->hqk", query_part, key_heads, preferred_element_type=jnp.float32
        ) * HEAD_DIM ** (-0.5)
        allowed = allowed_fn(first_row + jnp.arange(block_rows, dtype=jnp.int32))
        scores = jnp.where(allowed[None], scores, -1e30)
        row_max = jnp.max(scores, axis=-1, keepdims=True)
        expo = jnp.exp(scores - row_max)
        probabilities = (expo / jnp.sum(expo, axis=-1, keepdims=True)).astype(jnp.bfloat16)
        return jnp.einsum(
            "hqk,khe->qhe", probabilities, value_heads, preferred_element_type=jnp.float32
        ).astype(jnp.bfloat16)

    starts = jnp.arange(block_count, dtype=jnp.int32) * block_rows
    joined = lax.map(one_block, (query_blocks, starts))
    return joined.reshape(length, head_width)


def heads_to_rows(heads, seq_count):
    length, width = heads.shape
    rows = length // seq_count
    blocks = heads.reshape(seq_count, rows, width)
    swapped = lax.all_to_all(blocks, "seq", split_axis=0, concat_axis=0, tiled=True)
    return swapped.transpose(1, 0, 2).reshape(rows, seq_count * width)


def attend_causal(queries, key_rows, value_rows, allowed_fn):
    length = queries.shape[0]
    head_width = queries.shape[1]
    head_count = head_width // HEAD_DIM
    block_rows = min(512, length)
    block_count = length // block_rows
    key_heads = key_rows.reshape(length, head_count, HEAD_DIM)
    value_heads = value_rows.reshape(length, head_count, HEAD_DIM)
    outputs = []
    for block in range(block_count):
        first_row = block * block_rows
        key_end = first_row + block_rows
        query_part = queries[first_row:key_end].reshape(block_rows, head_count, HEAD_DIM)
        scores = jnp.einsum(
            "qhe,khe->hqk", query_part, key_heads[:key_end], preferred_element_type=jnp.float32
        ) * HEAD_DIM ** (-0.5)
        allowed = allowed_fn(first_row + jnp.arange(block_rows, dtype=jnp.int32))[:, :key_end]
        scores = jnp.where(allowed[None], scores, -1e30)
        row_max = jnp.max(scores, axis=-1, keepdims=True)
        expo = jnp.exp(scores - row_max)
        probabilities = (expo / jnp.sum(expo, axis=-1, keepdims=True)).astype(jnp.bfloat16)
        outputs.append(
            jnp.einsum(
                "hqk,khe->qhe", probabilities, value_heads[:key_end], preferred_element_type=jnp.float32
            ).astype(jnp.bfloat16)
        )
    return jnp.concatenate(outputs, axis=0).reshape(length, head_width)


def per_device(
    patches,
    vis_gain,
    vis_qkv,
    vis_out,
    merge_gain,
    merge_w,
    image_blocks,
    dest_group,
    slot_rows,
    prompt_len,
    text_emb,
    txt_gain,
    txt_qkv,
    txt_out,
):
    seq_count = lax.axis_size("seq")
    groups = lax.axis_size("grp")
    token_count = patches.shape[0]
    model_width = patches.shape[1]
    group_patches = token_count * seq_count
    vis_out_full = lax.all_gather(vis_out, "seq", axis=0, tiled=True)
    vis_normed = layer_norm_fused(patches, vis_gain)
    vis_proj = projector(vis_qkv, lax.all_gather(vis_normed, "seq", axis=0, tiled=True))
    bounds = jnp.cumsum(image_blocks[0])[:-1]

    def segment(indices):
        return jnp.sum(((indices // 4)[:, None] >= bounds[None, :]).astype(jnp.int32), axis=1)

    key_segments = segment(jnp.arange(group_patches, dtype=jnp.int32))

    def vis_allowed(row_indices):
        return segment(row_indices)[:, None] == key_segments[None, :]

    vis_heads = attend_local(vis_proj[0], vis_proj[1], vis_proj[2], vis_allowed)
    vis_heads, txt_out = lax.optimization_barrier((vis_heads, txt_out))
    txt_out_full = lax.all_gather(txt_out, "seq", axis=0, tiled=True)
    vis_attn = jnp.dot(
        heads_to_rows(vis_heads, seq_count), vis_out_full, preferred_element_type=jnp.float32
    )
    residual_sum = patches.astype(jnp.float32) + vis_attn
    merged_in = (
        layer_norm(residual_sum, merge_gain)
        .astype(jnp.bfloat16)
        .reshape(token_count // 4, 4 * model_width)
    )
    feature_slices = lax.all_to_all(merged_in, "seq", split_axis=1, concat_axis=0, tiled=True)
    merge_partial = jnp.dot(feature_slices, merge_w, preferred_element_type=jnp.float32)
    merge_parts = lax.all_to_all(
        merge_partial.astype(jnp.bfloat16).reshape(seq_count, -1, model_width),
        "seq",
        split_axis=0,
        concat_axis=0,
        tiled=True,
    )
    visual = jnp.sum(merge_parts.astype(jnp.float32), axis=0).astype(jnp.bfloat16)
    dest_rows = dest_group[:, 0]
    merged_rows = dest_rows.shape[0]
    capacity = max(2, 2 * merged_rows // groups)
    onehot = (dest_rows[:, None] == jnp.arange(groups, dtype=jnp.int32)[None, :]).astype(jnp.int32)
    slot_rank = jnp.sum((jnp.cumsum(onehot, axis=0) - 1) * onehot, axis=1)
    selector = (
        (dest_rows[None, None, :] == jnp.arange(groups, dtype=jnp.int32)[:, None, None])
        & (slot_rank[None, None, :] == jnp.arange(capacity, dtype=jnp.int32)[None, :, None])
    ).astype(jnp.bfloat16)
    outgoing = jnp.einsum(
        "gct,td->gcd", selector, visual, preferred_element_type=jnp.float32
    ).astype(jnp.bfloat16)
    arrived_flags = jnp.sum(selector.astype(jnp.float32), axis=2).astype(jnp.bfloat16)
    flag_row = jnp.pad(arrived_flags, ((0, 0), (0, model_width - capacity)))[:, None, :]
    payload = lax.all_to_all(
        jnp.concatenate([outgoing, flag_row], axis=1), "grp", split_axis=0, concat_axis=0, tiled=True
    )
    incoming = payload[:, :capacity, :]
    arrived = payload[:, capacity, :capacity]
    prompt_rows = text_emb.shape[0]
    slot_targets = slot_rows[0, 0, : groups * capacity]
    placement_map = (
        slot_targets[None, :] == jnp.arange(prompt_rows, dtype=jnp.int32)[:, None]
    ).astype(jnp.bfloat16)
    placement_map = placement_map * arrived.reshape(1, groups * capacity)
    replaced = jnp.sum(placement_map.astype(jnp.float32), axis=1, keepdims=True)
    placed = jnp.dot(
        placement_map,
        incoming.reshape(groups * capacity, model_width),
        preferred_element_type=jnp.float32,
    )
    hidden = (text_emb.astype(jnp.float32) * (1.0 - replaced) + placed).astype(jnp.bfloat16)
    txt_normed = rms_norm(hidden, txt_gain).astype(jnp.bfloat16)
    txt_normed, txt_out_full = lax.optimization_barrier((txt_normed, txt_out_full))
    txt_proj = projector(txt_qkv, lax.all_gather(txt_normed, "seq", axis=0, tiled=True))
    length = prompt_len[0]
    key_positions = jnp.arange(prompt_rows * seq_count, dtype=jnp.int32)

    def txt_allowed(row_indices):
        return (key_positions[None, :] <= row_indices[:, None]) & (key_positions[None, :] < length)

    txt_heads = attend_causal(txt_proj[0], txt_proj[1], txt_proj[2], txt_allowed)
    txt_attn = jnp.dot(
        heads_to_rows(txt_heads, seq_count), txt_out_full, preferred_element_type=jnp.float32
    )
    return hidden.astype(jnp.float32) + txt_attn


def solution(mesh):
    in_specs = (
        P(("grp", "seq"), None),
        P(),
        P(None, None, "seq"),
        P("seq", None),
        P(),
        P("seq", None),
        P("grp", None),
        P(("grp", "seq"), None),
        P("grp", "seq", None),
        P("grp"),
        P(("grp", "seq"), None),
        P(),
        P(None, None, "seq"),
        P("seq", None),
    )
    out_specs = P(("grp", "seq"), None)
    return jax.shard_map(
        per_device, mesh=mesh, in_specs=in_specs, out_specs=out_specs, check_vma=False
    )
```

```python
import jax
import jax.numpy as jnp
from jax.experimental import pallas as pl
from jax.experimental.pallas import tpu as pltpu
from jax import lax
from jax.sharding import PartitionSpec as P

HEAD_DIM = 104


def layer_norm(row_block, scale_gain):
    values_f = row_block.astype(jnp.float32)
    row_mean = jnp.mean(values_f, axis=-1, keepdims=True)
    centred = values_f - row_mean
    variance = jnp.mean(centred * centred, axis=-1, keepdims=True)
    return centred * lax.rsqrt(variance + 1e-06) * scale_gain


def layer_norm_kernel(x_ref, g_ref, o_ref):
    values_f = x_ref[...].astype(jnp.float32)
    row_mean = jnp.mean(values_f, axis=-1, keepdims=True)
    centred = values_f - row_mean
    variance = jnp.mean(centred * centred, axis=-1, keepdims=True)
    o_ref[...] = (centred * lax.rsqrt(variance + 1e-06) * g_ref[...][None, :]).astype(o_ref.dtype)


def layer_norm_fused(row_block, scale_gain):
    rows, width = row_block.shape
    return pl.pallas_call(
        layer_norm_kernel,
        out_shape=jax.ShapeDtypeStruct((rows, width), jnp.bfloat16),
        in_specs=[pl.BlockSpec(memory_space=pltpu.VMEM)] * 2,
        out_specs=pl.BlockSpec(memory_space=pltpu.VMEM),
        cost_estimate=pl.CostEstimate(
            flops=8 * rows * width, transcendentals=rows, bytes_accessed=4 * rows * width + 4 * width
        ),
    )(row_block, scale_gain)


def rms_norm(row_block, scale_gain):
    values_f = row_block.astype(jnp.float32)
    return (
        values_f
        * lax.rsqrt(jnp.mean(values_f * values_f, axis=-1, keepdims=True) + 1e-06)
        * scale_gain
    )


def projector(weights, shard_piece):
    count, width, head_width = weights.shape
    packed = weights.transpose(1, 0, 2).reshape(width, count * head_width)
    joined = jnp.dot(shard_piece, packed, preferred_element_type=jnp.float32).astype(jnp.bfloat16)
    return joined.reshape(shard_piece.shape[0], count, head_width).transpose(1, 0, 2)


def attend_local(queries, key_rows, value_rows, allowed_fn):
    length = queries.shape[0]
    head_width = queries.shape[1]
    head_count = head_width // HEAD_DIM
    block_rows = min(512, length)
    block_count = length // block_rows
    query_blocks = queries.reshape(block_count, block_rows, head_count, HEAD_DIM)
    key_heads = key_rows.reshape(length, head_count, HEAD_DIM)
    value_heads = value_rows.reshape(length, head_count, HEAD_DIM)

    def one_block(block_item):
        query_part, first_row = block_item
        scores = jnp.einsum(
            "qhe,khe->hqk", query_part, key_heads, preferred_element_type=jnp.float32
        ) * HEAD_DIM ** (-0.5)
        allowed = allowed_fn(first_row + jnp.arange(block_rows, dtype=jnp.int32))
        scores = jnp.where(allowed[None], scores, -1e30)
        row_max = jnp.max(scores, axis=-1, keepdims=True)
        expo = jnp.exp(scores - row_max)
        probabilities = (expo / jnp.sum(expo, axis=-1, keepdims=True)).astype(jnp.bfloat16)
        return jnp.einsum(
            "hqk,khe->qhe", probabilities, value_heads, preferred_element_type=jnp.float32
        ).astype(jnp.bfloat16)

    starts = jnp.arange(block_count, dtype=jnp.int32) * block_rows
    joined = lax.map(one_block, (query_blocks, starts))
    return joined.reshape(length, head_width)


def heads_to_rows(heads, seq_count):
    length, width = heads.shape
    rows = length // seq_count
    blocks = heads.reshape(seq_count, rows, width)
    swapped = lax.all_to_all(blocks, "seq", split_axis=0, concat_axis=0, tiled=True)
    return swapped.transpose(1, 0, 2).reshape(rows, seq_count * width)


def attend_causal(queries, key_rows, value_rows, allowed_fn):
    length = queries.shape[0]
    head_width = queries.shape[1]
    head_count = head_width // HEAD_DIM
    block_rows = min(512, length)
    block_count = length // block_rows
    key_heads = key_rows.reshape(length, head_count, HEAD_DIM)
    value_heads = value_rows.reshape(length, head_count, HEAD_DIM)
    outputs = []
    for block in range(block_count):
        first_row = block * block_rows
        key_end = first_row + block_rows
        query_part = queries[first_row:key_end].reshape(block_rows, head_count, HEAD_DIM)
        scores = jnp.einsum(
            "qhe,khe->hqk", query_part, key_heads[:key_end], preferred_element_type=jnp.float32
        ) * HEAD_DIM ** (-0.5)
        allowed = allowed_fn(first_row + jnp.arange(block_rows, dtype=jnp.int32))[:, :key_end]
        scores = jnp.where(allowed[None], scores, -1e30)
        row_max = jnp.max(scores, axis=-1, keepdims=True)
        expo = jnp.exp(scores - row_max)
        probabilities = (expo / jnp.sum(expo, axis=-1, keepdims=True)).astype(jnp.bfloat16)
        outputs.append(
            jnp.einsum(
                "hqk,khe->qhe", probabilities, value_heads[:key_end], preferred_element_type=jnp.float32
            ).astype(jnp.bfloat16)
        )
    return jnp.concatenate(outputs, axis=0).reshape(length, head_width)


def per_device(
    patches,
    vis_gain,
    vis_qkv,
    vis_out,
    merge_gain,
    merge_w,
    image_blocks,
    dest_group,
    slot_rows,
    prompt_len,
    text_emb,
    txt_gain,
    txt_qkv,
    txt_out,
):
    seq_count = lax.axis_size("seq")
    groups = lax.axis_size("grp")
    token_count = patches.shape[0]
    model_width = patches.shape[1]
    group_patches = token_count * seq_count
    vis_out_full = lax.all_gather(vis_out, "seq", axis=0, tiled=True)
    vis_normed = layer_norm_fused(patches, vis_gain)
    vis_proj = projector(vis_qkv, lax.all_gather(vis_normed, "seq", axis=0, tiled=True))
    bounds = jnp.cumsum(image_blocks[0])[:-1]

    def segment(indices):
        return jnp.sum(((indices // 4)[:, None] >= bounds[None, :]).astype(jnp.int32), axis=1)

    key_segments = segment(jnp.arange(group_patches, dtype=jnp.int32))

    def vis_allowed(row_indices):
        return segment(row_indices)[:, None] == key_segments[None, :]

    vis_heads = attend_local(vis_proj[0], vis_proj[1], vis_proj[2], vis_allowed)
    vis_heads, txt_out = lax.optimization_barrier((vis_heads, txt_out))
    txt_out_full = lax.all_gather(txt_out, "seq", axis=0, tiled=True)
    vis_attn = jnp.dot(
        heads_to_rows(vis_heads, seq_count), vis_out_full, preferred_element_type=jnp.float32
    )
    residual_sum = patches.astype(jnp.float32) + vis_attn
    merged_in = (
        layer_norm(residual_sum, merge_gain)
        .astype(jnp.bfloat16)
        .reshape(token_count // 4, 4 * model_width)
    )
    feature_slices = lax.all_to_all(merged_in, "seq", split_axis=1, concat_axis=0, tiled=True)
    merge_partial = jnp.dot(feature_slices, merge_w, preferred_element_type=jnp.float32)
    merge_parts = lax.all_to_all(
        merge_partial.astype(jnp.bfloat16).reshape(seq_count, -1, model_width),
        "seq",
        split_axis=0,
        concat_axis=0,
        tiled=True,
    )
    visual = jnp.sum(merge_parts.astype(jnp.float32), axis=0).astype(jnp.bfloat16)
    dest_rows = dest_group[:, 0]
    merged_rows = dest_rows.shape[0]
    capacity = max(2, 2 * merged_rows // groups)
    onehot = (dest_rows[:, None] == jnp.arange(groups, dtype=jnp.int32)[None, :]).astype(jnp.int32)
    slot_rank = jnp.sum((jnp.cumsum(onehot, axis=0) - 1) * onehot, axis=1)
    selector = (
        (dest_rows[None, None, :] == jnp.arange(groups, dtype=jnp.int32)[:, None, None])
        & (slot_rank[None, None, :] == jnp.arange(capacity, dtype=jnp.int32)[None, :, None])
    ).astype(jnp.bfloat16)
    arrived_flags = jnp.sum(selector.astype(jnp.float32), axis=2).astype(jnp.bfloat16)
    selector_ext = jnp.concatenate(
        [
            jnp.pad(selector, ((0, 0), (0, 0), (0, capacity))),
            jnp.pad(arrived_flags, ((0, 0), (merged_rows, 0)))[:, None, :],
        ],
        axis=1,
    )
    visual_ext = jnp.concatenate(
        [visual, jnp.eye(capacity, model_width, dtype=jnp.bfloat16)], axis=0
    )
    outgoing = jnp.einsum(
        "gct,td->gcd", selector_ext, visual_ext, preferred_element_type=jnp.float32
    ).astype(jnp.bfloat16)
    payload = lax.all_to_all(outgoing, "grp", split_axis=0, concat_axis=0, tiled=True)
    incoming = payload[:, :capacity, :]
    arrived = payload[:, capacity, :capacity]
    prompt_rows = text_emb.shape[0]
    slot_targets = slot_rows[0, 0, : groups * capacity]
    placement_map = (
        slot_targets[None, :] == jnp.arange(prompt_rows, dtype=jnp.int32)[:, None]
    ).astype(jnp.bfloat16)
    placement_map = placement_map * arrived.reshape(1, groups * capacity)
    replaced = jnp.sum(placement_map.astype(jnp.float32), axis=1, keepdims=True)
    placed = jnp.dot(
        placement_map,
        incoming.reshape(groups * capacity, model_width),
        preferred_element_type=jnp.float32,
    )
    hidden = (text_emb.astype(jnp.float32) * (1.0 - replaced) + placed).astype(jnp.bfloat16)
    txt_normed = rms_norm(hidden, txt_gain).astype(jnp.bfloat16)
    txt_normed, txt_out_full = lax.optimization_barrier((txt_normed, txt_out_full))
    txt_proj = projector(txt_qkv, lax.all_gather(txt_normed, "seq", axis=0, tiled=True))
    length = prompt_len[0]
    key_positions = jnp.arange(prompt_rows * seq_count, dtype=jnp.int32)

    def txt_allowed(row_indices):
        return (key_positions[None, :] <= row_indices[:, None]) & (key_positions[None, :] < length)

    txt_heads = attend_causal(txt_proj[0], txt_proj[1], txt_proj[2], txt_allowed)
    txt_attn = jnp.dot(
        heads_to_rows(txt_heads, seq_count), txt_out_full, preferred_element_type=jnp.float32
    )
    return hidden.astype(jnp.float32) + txt_attn


def solution(mesh):
    in_specs = (
        P(("grp", "seq"), None),
        P(),
        P(None, None, "seq"),
        P("seq", None),
        P(),
        P("seq", None),
        P("grp", None),
        P(("grp", "seq"), None),
        P("grp", "seq", None),
        P("grp"),
        P(("grp", "seq"), None),
        P(),
        P(None, None, "seq"),
        P("seq", None),
    )
    out_specs = P(("grp", "seq"), None)
    return jax.shard_map(
        per_device, mesh=mesh, in_specs=in_specs, out_specs=out_specs, check_vma=False
    )
```
